256 devices in a mesh: gx: 8 (over z), gy: 32 (over y, x, core).
Axes of the slice: x: 4, y: 4, z: 8, core: 2. Of those that a mesh axis runs over, the one named last changes fastest.
Arguments:
- lengths: int32 [17], replicated, may hold values from 16 to 16384, as said below
- page_table: int32 [1169], replicated, may hold values from 0 to 1287, as said below
- projected: bfloat16 [18432, 9216], P('gx', 'gy'), may hold values from -8 to 8
- residual: bfloat16 [18432, 3072], P('gx', 'gy'), may hold values from -6 to 6
- out_weight: bfloat16 [3072, 3072], P('gx', 'gy'), may hold values from -0.109375 to 0.109375
Outputs:
- hidden: bfloat16 [18432, 3072], P('gx', 'gy')
- cache_pages: bfloat16 [1288, 32, 3072], P('gx', 'gy')
The draws below stay inside these ranges and needn't reach their ends.
Inputs may be any that keep to these rules, and one draw needn't show every extreme that they name: `lengths`: one prompt of 16384 tokens at a place drawn from the seed and 16 short prompts of 16 to 240 tokens; they sum to 18432. `page_table`: entry g is the physical page of logical page g (the pages of each prompt in order, 16 tokens each, prompts in packing order). Distinct logical pages in use get distinct physical pages, and such a page lies in [d * 161, (d + 1) * 161) where d is the index of gx whose tokens hold the page's first token. Entries past the last logical page in use are arbitrary; the last two entries are never in use and hold 0 and 1287.
All inputs are finite; a program needn't handle non-finite values.
Results may differ from the reference program's by a relative error of at most 0.012.
The reference program's roundings to bfloat16 on the way count: a program that leaves them out, or rounds other values in their place, can miss the bound.
Values may be sent and summed in bfloat16 or wider, within the bound.
No kernel may reach another device: no remote copies, remote signals or barrier semaphores. Data moves between devices by JAX's collectives and lax.ppermute only.
A program may use at most 128 MiB of HBM per device.

```python
import math
import jax
import jax.numpy as jnp
from jax import lax

D = 3072
H = 32
HD = 96
TOK_DEV = 2304
PAGE = 16
TOKENS = 18432
LONG = 16384
SHORTS = 16
NSEQ = 17
PG_DEV = 161
NP = 1288
MAXLOG = 1169
N_GX = 8


def prompt_lengths(key):
    folded = jax.random.fold_in(key, 11)
    pick_key, order_key, slot_key = jax.random.split(folded, 3)
    pair_count = SHORTS // 2
    offsets = jax.random.randint(pick_key, (max(pair_count, 1),), 0, 225).astype(jnp.int32)
    offsets = offsets.at[0].set(0)[:pair_count]
    single = jnp.full((SHORTS - 2 * pair_count,), 128, jnp.int32)
    shorts = jnp.concatenate([16 + offsets, 240 - offsets, single]).astype(jnp.int32)
    shorts = shorts[jax.random.permutation(order_key, SHORTS)]
    long_slot = jax.random.randint(slot_key, (), 0, NSEQ)
    slot_index = jnp.arange(NSEQ, dtype=jnp.int32)
    earlier = shorts[jnp.clip(slot_index, 0, SHORTS - 1)]
    after_long = shorts[jnp.clip(slot_index - 1, 0, SHORTS - 1)]
    return jnp.where(slot_index < long_slot, earlier, jnp.where(slot_index == long_slot, LONG, after_long)).astype(jnp.int32)


def draw_lengths(key, part):
    return prompt_lengths(key)


def draw_page_table(key, part):
    lengths = prompt_lengths(key)
    ends_at = jnp.cumsum(lengths)
    starts_at = ends_at - lengths
    page_count = (lengths + PAGE - 1) // PAGE
    page_end = jnp.cumsum(page_count)
    page_start = page_end - page_count
    logical = jnp.arange(MAXLOG, dtype=jnp.int32)
    prompt = jnp.sum((page_end[None, :] <= logical[:, None]).astype(jnp.int32), axis=1)
    in_use = prompt < NSEQ
    prompt = jnp.minimum(prompt, NSEQ - 1)
    first_token = starts_at[prompt] + PAGE * (logical - page_start[prompt])
    holder = jnp.where(in_use, first_token // TOK_DEV, N_GX)
    device_ids = jnp.arange(N_GX, dtype=jnp.int32)
    holder_first = jnp.sum((holder[None, :] < device_ids[:, None]).astype(jnp.int32), axis=1)
    clipped = jnp.minimum(holder, N_GX - 1)
    within = jnp.clip(logical - holder_first[clipped], 0, PG_DEV - 1)
    shuffle_key, spare_key = jax.random.split(jax.random.fold_in(key, 12))
    orders = jax.vmap(lambda single_key: jax.random.permutation(single_key, PG_DEV))(jax.random.split(shuffle_key, N_GX))
    physical = clipped * PG_DEV + orders[clipped, within]
    spare = jax.random.randint(spare_key, (MAXLOG,), 0, NP).astype(jnp.int32)
    spare = spare.at[MAXLOG - 1].set(NP - 1)
    spare = spare.at[MAXLOG - 2].set(0)
    return jnp.where(in_use, physical, spare).astype(jnp.int32)


def draw_projected(key, part):
    folded = jax.random.fold_in(key, 21)
    base_key = jax.random.fold_in(folded, 0)
    full_shape = (TOKENS, H, 3, HD)
    drawn = jnp.clip(2.0 * jax.random.normal(base_key, full_shape, jnp.float32), -8.0, 8.0)
    return drawn.reshape(TOKENS, H * 3 * HD).astype(jnp.bfloat16)


def level_of(stream_key, extent, pieces, smallest, high):
    def one(axis_at, parts):
        draws = jax.random.uniform(jax.random.fold_in(jax.random.fold_in(stream_key, 6), axis_at), (parts,), jnp.float32, smallest / len(pieces), high / len(pieces))
        return jnp.repeat(jnp.exp(draws), extent[axis_at] // parts).reshape((-1,) + (1,) * (len(extent) - axis_at - 1))

    level = one(*pieces[0])
    for cut in pieces[1:]:
        level = level * one(*cut)
    return level


def noise(stream_key, extent, spread, bound, pieces=(), held_as=jnp.bfloat16):
    array = spread * jax.random.normal(stream_key, extent, jnp.float32)
    if pieces:
        array = array * level_of(stream_key, extent, pieces, -0.22, 0.18)
    return jnp.clip(array, -bound, bound).astype(held_as)


def setup_inputs(seed: int = 0) -> dict:
    keys = jax.random.split(jax.random.key(seed), 6)
    return {
        "lengths": draw_lengths(jax.random.fold_in(keys[5], 71), 0),
        "page_table": draw_page_table(jax.random.fold_in(keys[5], 71), 0),
        "projected": draw_projected(jax.random.fold_in(keys[5], 71), 0),
        "residual": noise(keys[3], (TOKENS, D), 1.0, 6.0, ((0, 8), (1, 32))),
        "out_weight": noise(keys[4], (H * HD, D), (H * HD) ** -0.5, 0.109375, ((0, 8), (1, 32))),
    }


def packed_layout(lengths):
    ends_at = jnp.cumsum(lengths)
    starts_at = ends_at - lengths
    token_index = jnp.arange(TOKENS, dtype=jnp.int32)
    segment = lax.optimization_barrier(jnp.sum((ends_at[None, :] <= token_index[:, None]).astype(jnp.int32), axis=1))
    position = token_index - starts_at[segment]
    return (segment, position)

def rotate(values, position):
    half_size = HD // 2
    inverse = 10000.0 ** (-(jnp.arange(half_size, dtype=jnp.float32) * 2.0) / HD)
    angle = position.astype(jnp.float32)[:, None, None] * inverse[None, None, :]
    cosine = jnp.cos(angle)
    sine_part = jnp.sin(angle)
    widened = values.astype(jnp.float32)
    front_half = widened[..., :half_size]
    back_half = widened[..., half_size:]
    turned = jnp.concatenate([front_half * cosine - back_half * sine_part, back_half * cosine + front_half * sine_part], axis=-1)
    return turned.astype(jnp.bfloat16)

def attend(queries, key_rows, values, segment):
    block_rows = TOKENS // 16
    score_scale = 1.0 / math.sqrt(HD)
    outputs = []
    for number in range(16):
        lower_row = number * block_rows
        upper_row = lower_row + block_rows
        scores = jnp.dot(queries[lower_row:upper_row], key_rows[:upper_row].T, preferred_element_type=jnp.float32) * score_scale
        query_index = jnp.arange(lower_row, upper_row, dtype=jnp.int32)
        key_index = jnp.arange(upper_row, dtype=jnp.int32)
        visible = (segment[lower_row:upper_row, None] == segment[None, :upper_row]) & (query_index[:, None] >= key_index[None, :])
        scores = jnp.where(visible, scores, -jnp.inf)
        largest = lax.optimization_barrier(jnp.max(scores, axis=1, keepdims=True))
        weights = jnp.where(visible, jnp.exp(scores - largest), 0.0)
        denominator = lax.optimization_barrier(jnp.sum(weights, axis=1, keepdims=True))
        blended = jnp.dot(weights.astype(jnp.bfloat16), values[:upper_row], preferred_element_type=jnp.float32) / denominator
        outputs.append(blended.astype(jnp.bfloat16))
    return jnp.concatenate(outputs, axis=0)

def reference(lengths, page_table, projected, residual, out_weight):
    segment, position = packed_layout(lengths)
    split_heads = projected.reshape(TOKENS, H, 3, HD)
    rotated_queries = rotate(split_heads[:, :, 0], position)
    rotated_keys = rotate(split_heads[:, :, 1], position)
    head_values = split_heads[:, :, 2]

    def one_head(operands):
        return attend(operands[0], operands[1], operands[2], segment)
    attended = lax.map(one_head, (jnp.swapaxes(rotated_queries, 0, 1), jnp.swapaxes(rotated_keys, 0, 1), jnp.swapaxes(head_values, 0, 1)))
    attended = jnp.swapaxes(attended, 0, 1).reshape(TOKENS, H * HD)
    update = jnp.dot(attended, out_weight, preferred_element_type=jnp.float32)
    hidden = (residual.astype(jnp.float32) + update).astype(jnp.bfloat16)
    page_count = (lengths + PAGE - 1) // PAGE
    page_base = jnp.cumsum(page_count) - page_count
    logical = page_base[segment] + position // PAGE
    physical = page_table[logical]
    in_page = position % PAGE
    entries = jnp.concatenate([rotated_keys, head_values], axis=-1)
    cache_pages = jnp.zeros((NP, H, PAGE, 2 * HD), jnp.bfloat16)
    cache_pages = cache_pages.at[physical, :, in_page].set(entries)
    return (hidden, cache_pages.reshape(NP, H, PAGE * 2 * HD))
```

```python
from functools import partial
import math

import jax
import jax.numpy as jnp
from jax import lax
from jax.experimental import pallas as pl
from jax.experimental.pallas import tpu as pltpu
from jax.sharding import PartitionSpec as P

HD = 96
PAGE = 16
BQ = 256
BK = 768
NEG = -1e30


def passed_along(block, axis, distance):
    devices = range(lax.axis_size(axis))
    route = [(i - distance, i) for i in devices if i - distance in devices]
    return lax.ppermute(block, axis, route)


def segment_of(ends_at, token_index):
    return jnp.sum((ends_at[None, :] <= token_index[:, None]).astype(jnp.int32), axis=1)


def rotate(values, position):
    half_size = HD // 2
    inverse = 10000.0 ** (-(jnp.arange(half_size, dtype=jnp.float32) * 2.0) / HD)
    angle = position.astype(jnp.float32)[:, None, None] * inverse[None, None, :]
    cosine = jnp.cos(angle)
    sine_part = jnp.sin(angle)
    widened = values.astype(jnp.float32)
    front_half = widened[..., :half_size]
    back_half = widened[..., half_size:]
    turned = jnp.concatenate(
        [front_half * cosine - back_half * sine_part, back_half * cosine + front_half * sine_part],
        axis=-1,
    )
    return turned.astype(jnp.bfloat16)


def attention_kernel(table_ref, q_ref, lo_ref, kv_ref, *rest, has_init, finalize):
    if has_init:
        m_in, l_in, acc_in = rest[:3]
        rest = rest[3:]
    i = pl.program_id(0)
    b0 = table_ref[i * 8 + 0]
    b1 = table_ref[i * 8 + 1]
    b2 = table_ref[i * 8 + 2]
    b3 = table_ref[i * 8 + 3]
    q_first = table_ref[i * 8 + 4]
    key_offset = table_ref[i * 8 + 5]
    q = q_ref[...]
    lo = lo_ref[...]
    q_index = q_first + lax.broadcasted_iota(jnp.int32, (BQ, 1), 0)
    scale = 1.0 / math.sqrt(HD)

    def step(kb, carry, masked):
        m, l, acc = carry
        start = pl.multiple_of(kb * BK, BK)
        keys = kv_ref[pl.ds(start, BK), pl.ds(0, HD)]
        vals = kv_ref[pl.ds(start, BK), pl.ds(HD, HD)]
        s = lax.dot_general(q, keys, (((1,), (1,)), ((), ())), preferred_element_type=jnp.float32) * scale
        if masked:
            k_index = key_offset + start + lax.broadcasted_iota(jnp.int32, (1, BK), 1)
            visible = (k_index >= lo) & (k_index <= q_index)
            s = jnp.where(visible, s, NEG)
        m_new = jnp.maximum(m, jnp.max(s, axis=1, keepdims=True))
        p = jnp.exp(s - m_new)
        if masked:
            p = jnp.where(visible, p, 0.0)
        alpha = jnp.exp(m - m_new)
        l_new = l * alpha + jnp.sum(p, axis=1, keepdims=True)
        acc_new = acc * alpha + jnp.dot(p.astype(jnp.bfloat16), vals, preferred_element_type=jnp.float32)
        return (m_new, l_new, acc_new)

    if has_init:
        carry = (m_in[...], l_in[...], acc_in[...])
    else:
        carry = (
            jnp.full((BQ, 1), NEG, jnp.float32),
            jnp.zeros((BQ, 1), jnp.float32),
            jnp.zeros((BQ, HD), jnp.float32),
        )
    carry = lax.fori_loop(b0, b1, partial(step, masked=True), carry)
    carry = lax.fori_loop(b1, b2, partial(step, masked=False), carry)
    carry = lax.fori_loop(b2, b3, partial(step, masked=True), carry)
    m, l, acc = carry
    if finalize:
        (out_ref,) = rest
        out_ref[...] = (acc / l).astype(out_ref.dtype)
    else:
        m_out, l_out, acc_out = rest
        m_out[...] = m
        l_out[...] = l
        acc_out[...] = acc


def block_table(q_first_rows, lo_first, lo_last, key_offset, key_rows):
    q_last = q_first_rows + BQ - 1
    local_lo = jnp.clip(lo_first - key_offset, 0, key_rows)
    local_hi = jnp.clip(q_last + 1 - key_offset, 0, key_rows)
    b0 = local_lo // BK
    b3 = jnp.maximum((local_hi + BK - 1) // BK, b0)
    full_lo = (jnp.maximum(lo_last - key_offset, 0) + BK - 1) // BK
    full_hi = (q_first_rows + 1 - key_offset) // BK
    b1 = jnp.clip(full_lo, b0, b3)
    b2 = jnp.clip(full_hi, b1, b3)
    offsets = jnp.broadcast_to(key_offset, q_first_rows.shape)
    zero = jnp.zeros_like(b0)
    table = jnp.stack([b0, b1, b2, b3, q_first_rows, offsets, zero, zero], axis=1)
    return table.reshape(-1).astype(jnp.int32)


def attend(table, queries, lows, kv, state, finalize):
    rows = queries.shape[0]
    key_rows = kv.shape[0]
    grid = (rows // BQ,)
    row_spec = lambda width: pl.BlockSpec((BQ, width), lambda i, t: (i, 0))
    in_specs = [row_spec(HD), row_spec(1), pl.BlockSpec((key_rows, 2 * HD), lambda i, t: (0, 0))]
    operands = [queries, lows, kv]
    if state is not None:
        in_specs += [row_spec(1), row_spec(1), row_spec(HD)]
        operands += list(state)
    if finalize:
        out_shape = jax.ShapeDtypeStruct((rows, HD), jnp.bfloat16)
        out_specs = row_spec(HD)
    else:
        out_shape = (
            jax.ShapeDtypeStruct((rows, 1), jnp.float32),
            jax.ShapeDtypeStruct((rows, 1), jnp.float32),
            jax.ShapeDtypeStruct((rows, HD), jnp.float32),
        )
        out_specs = (row_spec(1), row_spec(1), row_spec(HD))
    kernel = partial(attention_kernel, has_init=state is not None, finalize=finalize)
    return pl.pallas_call(
        kernel,
        grid_spec=pltpu.PrefetchScalarGridSpec(
            num_scalar_prefetch=1,
            grid=grid,
            in_specs=in_specs,
            out_specs=out_specs,
        ),
        out_shape=out_shape,
        compiler_params=pltpu.CompilerParams(vmem_limit_bytes=48 * 1024 * 1024),
    )(table, *operands)


def per_device(lengths, page_table, projected, residual, out_weight):
    row_count = projected.shape[0]
    local_heads = projected.shape[1] // (3 * HD)
    group_size = lax.axis_size("gx")
    group_index = lax.axis_index("gx")
    first_row = group_index * row_count
    ends_at = jnp.cumsum(lengths)
    starts_at = ends_at - lengths
    own_index = first_row + jnp.arange(row_count, dtype=jnp.int32)
    own_segment = segment_of(ends_at, own_index)
    own_position = own_index - starts_at[own_segment]
    split_heads = projected.reshape(row_count, local_heads, 3, HD)
    rotated_queries = rotate(split_heads[:, :, 0], own_position)
    rotated_keys = rotate(split_heads[:, :, 1], own_position)
    key_value = jnp.concatenate([rotated_keys, split_heads[:, :, 2]], axis=-1)
    weight_columns = lax.all_gather(out_weight, "gx", axis=0, tiled=True)
    queries = rotated_queries.reshape(row_count, HD)
    local_kv = key_value.reshape(row_count, 2 * HD)
    queries, local_kv, weight_columns = lax.optimization_barrier((queries, local_kv, weight_columns))
    portion = lax.all_gather(local_kv, "gx", axis=0, tiled=True)
    key_count = portion.shape[0]

    lows = starts_at[own_segment]
    q_first_rows = first_row + jnp.arange(0, row_count, BQ, dtype=jnp.int32)
    lo_first = lows[0::BQ]
    lo_last = lows[BQ - 1 :: BQ]
    lows = lows.reshape(row_count, 1)
    own_table = block_table(q_first_rows, lo_first, lo_last, first_row, row_count)
    state = attend(own_table, queries, lows, local_kv, None, False)
    rest_table = block_table(q_first_rows, lo_first, lo_last, jnp.int32(0), jnp.minimum(first_row, key_count))
    attended = attend(rest_table, queries, lows, portion, state, True)

    update = jnp.dot(
        lax.all_gather(attended, "gy", axis=1, tiled=True),
        weight_columns,
        preferred_element_type=jnp.float32,
    )
    hidden = (residual.astype(jnp.float32) + update).astype(jnp.bfloat16)
    tail_rows = passed_along(key_value[: PAGE - 1], "gx", -1)
    extended = jnp.concatenate([key_value, tail_rows], axis=0)
    extended_index = first_row + jnp.arange(row_count + PAGE - 1, dtype=jnp.int32)
    extended_segment = jnp.minimum(segment_of(ends_at, extended_index), lengths.shape[0] - 1)
    extended_position = extended_index - starts_at[extended_segment]
    page_count = (lengths + PAGE - 1) // PAGE
    page_base = jnp.cumsum(page_count) - page_count
    logical = page_base[extended_segment] + extended_position // PAGE
    page_first = extended_index - extended_position % PAGE
    pages_held = row_count // PAGE + lengths.shape[0]
    owned = (page_first // row_count == group_index) & (extended_index < group_size * row_count)
    target = jnp.where(owned, page_table[logical] - group_index * pages_held, pages_held)
    cache_pages = jnp.zeros((pages_held, local_heads, PAGE, 2 * HD), jnp.bfloat16)
    cache_pages = cache_pages.at[target, :, extended_position % PAGE].set(extended, mode="drop")
    return (hidden, cache_pages.reshape(pages_held, local_heads, PAGE * 2 * HD))


def solution(mesh):
    placed = (P(), P(), P("gx", "gy"), P("gx", "gy"), P("gx", "gy"))
    return jax.shard_map(
        per_device,
        mesh=mesh,
        in_specs=placed,
        out_specs=(P("gx", "gy"), P("gx", "gy", None)),
        check_vma=False,
    )
```

```python
from functools import partial
import math

import jax
import jax.numpy as jnp
from jax import lax
from jax.experimental import pallas as pl
from jax.experimental.pallas import tpu as pltpu
from jax.sharding import PartitionSpec as P

HD = 96
PAGE = 16
BQ = 256
BK = 768
NEG = -1e30


def passed_along(block, axis, distance):
    devices = range(lax.axis_size(axis))
    route = [(i - distance, i) for i in devices if i - distance in devices]
    return lax.ppermute(block, axis, route)


def segment_of(ends_at, token_index):
    return jnp.sum((ends_at[None, :] <= token_index[:, None]).astype(jnp.int32), axis=1)


def rotate(values, position):
    half_size = HD // 2
    inverse = 10000.0 ** (-(jnp.arange(half_size, dtype=jnp.float32) * 2.0) / HD)
    angle = position.astype(jnp.float32)[:, None, None] * inverse[None, None, :]
    cosine = jnp.cos(angle)
    sine_part = jnp.sin(angle)
    widened = values.astype(jnp.float32)
    front_half = widened[..., :half_size]
    back_half = widened[..., half_size:]
    turned = jnp.concatenate(
        [front_half * cosine - back_half * sine_part, back_half * cosine + front_half * sine_part],
        axis=-1,
    )
    return turned.astype(jnp.bfloat16)


def attention_kernel(table_ref, q_ref, lo_ref, kv_ref, *rest, has_init, finalize, per_source):
    if has_init:
        m_in, l_in, acc_in = rest[:3]
        rest = rest[3:]
    i = pl.program_id(0)
    b0 = table_ref[i * 8 + 0]
    b1 = table_ref[i * 8 + 1]
    b2 = table_ref[i * 8 + 2]
    b3 = table_ref[i * 8 + 3]
    q_first = table_ref[i * 8 + 4]
    key_offset = table_ref[i * 8 + 5]
    q = q_ref[...]
    lo = lo_ref[...]
    q_index = q_first + lax.broadcasted_iota(jnp.int32, (BQ, 1), 0)
    scale = 1.0 / math.sqrt(HD)

    def step(kb, carry, masked):
        m, l, acc = carry
        start = pl.multiple_of(kb * BK, BK)
        source = kb // per_source
        within = pl.multiple_of((kb % per_source) * BK, BK)
        keys = kv_ref[source, pl.ds(within, BK), pl.ds(0, HD)]
        vals = kv_ref[source, pl.ds(within, BK), pl.ds(HD, HD)]
        s = lax.dot_general(q, keys, (((1,), (1,)), ((), ())), preferred_element_type=jnp.float32) * scale
        if masked:
            k_index = key_offset + start + lax.broadcasted_iota(jnp.int32, (1, BK), 1)
            visible = (k_index >= lo) & (k_index <= q_index)
            s = jnp.where(visible, s, NEG)
        m_new = jnp.maximum(m, jnp.max(s, axis=1, keepdims=True))
        p = jnp.exp(s - m_new)
        if masked:
            p = jnp.where(visible, p, 0.0)
        alpha = jnp.exp(m - m_new)
        l_new = l * alpha + jnp.sum(p, axis=1, keepdims=True)
        acc_new = acc * alpha + jnp.dot(p.astype(jnp.bfloat16), vals, preferred_element_type=jnp.float32)
        return (m_new, l_new, acc_new)

    if has_init:
        carry = (m_in[...], l_in[...], acc_in[...])
    else:
        carry = (
            jnp.full((BQ, 1), NEG, jnp.float32),
            jnp.zeros((BQ, 1), jnp.float32),
            jnp.zeros((BQ, HD), jnp.float32),
        )
    carry = lax.fori_loop(b0, b1, partial(step, masked=True), carry)
    carry = lax.fori_loop(b1, b2, partial(step, masked=False), carry)
    carry = lax.fori_loop(b2, b3, partial(step, masked=True), carry)
    m, l, acc = carry
    if finalize:
        (out_ref,) = rest
        out_ref[...] = (acc / l).astype(out_ref.dtype)
    else:
        m_out, l_out, acc_out = rest
        m_out[...] = m
        l_out[...] = l
        acc_out[...] = acc


def block_table(q_first_rows, lo_first, lo_last, key_offset, key_rows):
    q_last = q_first_rows + BQ - 1
    local_lo = jnp.clip(lo_first - key_offset, 0, key_rows)
    local_hi = jnp.clip(q_last + 1 - key_offset, 0, key_rows)
    b0 = local_lo // BK
    b3 = jnp.maximum((local_hi + BK - 1) // BK, b0)
    full_lo = (jnp.maximum(lo_last - key_offset, 0) + BK - 1) // BK
    full_hi = (q_first_rows + 1 - key_offset) // BK
    b1 = jnp.clip(full_lo, b0, b3)
    b2 = jnp.clip(full_hi, b1, b3)
    offsets = jnp.broadcast_to(key_offset, q_first_rows.shape)
    zero = jnp.zeros_like(b0)
    table = jnp.stack([b0, b1, b2, b3, q_first_rows, offsets, zero, zero], axis=1)
    return table.reshape(-1).astype(jnp.int32)


def attend(table, queries, lows, kv, state, finalize):
    rows = queries.shape[0]
    grid = (rows // BQ,)
    row_spec = lambda width: pl.BlockSpec((BQ, width), lambda i, t: (i, 0))
    in_specs = [row_spec(HD), row_spec(1), pl.BlockSpec(kv.shape, lambda i, t: (0, 0, 0))]
    operands = [queries, lows, kv]
    if state is not None:
        in_specs += [row_spec(1), row_spec(1), row_spec(HD)]
        operands += list(state)
    if finalize:
        out_shape = jax.ShapeDtypeStruct((rows, HD), jnp.bfloat16)
        out_specs = row_spec(HD)
    else:
        out_shape = (
            jax.ShapeDtypeStruct((rows, 1), jnp.float32),
            jax.ShapeDtypeStruct((rows, 1), jnp.float32),
            jax.ShapeDtypeStruct((rows, HD), jnp.float32),
        )
        out_specs = (row_spec(1), row_spec(1), row_spec(HD))
    kernel = partial(attention_kernel, has_init=state is not None, finalize=finalize, per_source=rows // BK)
    return pl.pallas_call(
        kernel,
        grid_spec=pltpu.PrefetchScalarGridSpec(
            num_scalar_prefetch=1,
            grid=grid,
            in_specs=in_specs,
            out_specs=out_specs,
        ),
        out_shape=out_shape,
        compiler_params=pltpu.CompilerParams(vmem_limit_bytes=48 * 1024 * 1024),
    )(table, *operands)


def per_device(lengths, page_table, projected, residual, out_weight):
    row_count = projected.shape[0]
    local_heads = projected.shape[1] // (3 * HD)
    group_size = lax.axis_size("gx")
    group_index = lax.axis_index("gx")
    first_row = group_index * row_count
    ends_at = jnp.cumsum(lengths)
    starts_at = ends_at - lengths
    own_index = first_row + jnp.arange(row_count, dtype=jnp.int32)
    own_segment = segment_of(ends_at, own_index)
    own_position = own_index - starts_at[own_segment]
    split_heads = projected.reshape(row_count, local_heads, 3, HD)
    rotated_queries = rotate(split_heads[:, :, 0], own_position)
    rotated_keys = rotate(split_heads[:, :, 1], own_position)
    key_value = jnp.concatenate([rotated_keys, split_heads[:, :, 2]], axis=-1)
    queries = rotated_queries.reshape(row_count, HD)
    local_kv = key_value.reshape(row_count, 2 * HD)
    weight_rows = out_weight.reshape(-1, 2 * HD)
    gathered = lax.all_gather(jnp.concatenate([local_kv, weight_rows], axis=0)[None], "gx", axis=0, tiled=True)
    weight_columns = gathered[:, row_count:].reshape(-1, out_weight.shape[1])
    key_count = group_size * row_count

    lows = starts_at[own_segment]
    q_first_rows = first_row + jnp.arange(0, row_count, BQ, dtype=jnp.int32)
    lo_first = lows[0::BQ]
    lo_last = lows[BQ - 1 :: BQ]
    lows = lows.reshape(row_count, 1)
    own_table = block_table(q_first_rows, lo_first, lo_last, first_row, row_count)
    state = attend(own_table, queries, lows, local_kv[None], None, False)

    tail_rows = passed_along(key_value[: PAGE - 1], "gx", -1)
    extended = jnp.concatenate([key_value, tail_rows], axis=0)
    extended_index = first_row + jnp.arange(row_count + PAGE - 1, dtype=jnp.int32)
    extended_segment = jnp.minimum(segment_of(ends_at, extended_index), lengths.shape[0] - 1)
    extended_position = extended_index - starts_at[extended_segment]
    page_count = (lengths + PAGE - 1) // PAGE
    page_base = jnp.cumsum(page_count) - page_count
    logical = page_base[extended_segment] + extended_position // PAGE
    page_first = extended_index - extended_position % PAGE
    pages_held = row_count // PAGE + lengths.shape[0]
    owned = (page_first // row_count == group_index) & (extended_index < group_size * row_count)
    target = jnp.where(owned, page_table[logical] - group_index * pages_held, pages_held)
    cache_pages = jnp.zeros((pages_held, local_heads, PAGE, 2 * HD), jnp.bfloat16)
    cache_pages = cache_pages.at[target, :, extended_position % PAGE].set(extended, mode="drop")

    gathered, cache_pages, state = lax.optimization_barrier((gathered, cache_pages, state))
    rest_table = block_table(q_first_rows, lo_first, lo_last, jnp.int32(0), jnp.minimum(first_row, key_count))
    attended = attend(rest_table, queries, lows, gathered, state, True)

    update = jnp.dot(
        lax.all_gather(attended, "gy", axis=1, tiled=True),
        weight_columns,
        preferred_element_type=jnp.float32,
    )
    hidden = (residual.astype(jnp.float32) + update).astype(jnp.bfloat16)
    return (hidden, cache_pages.reshape(pages_held, local_heads, PAGE * 2 * HD))


def solution(mesh):
    placed = (P(), P(), P("gx", "gy"), P("gx", "gy"), P("gx", "gy"))
    return jax.shard_map(
        per_device,
        mesh=mesh,
        in_specs=placed,
        out_specs=(P("gx", "gy"), P("gx", "gy", None)),
        check_vma=False,
    )
```

```python
from functools import partial
import math

import jax
import jax.numpy as jnp
from jax import lax
from jax.experimental import pallas as pl
from jax.experimental.pallas import tpu as pltpu
from jax.sharding import PartitionSpec as P

HD = 96
PAGE = 16
BQ = 256
BK = 768
CHUNK_BLOCKS = 3
NEG = -1e30


def passed_along(block, axis, distance):
    devices = range(lax.axis_size(axis))
    route = [(i - distance, i) for i in devices if i - distance in devices]
    return lax.ppermute(block, axis, route)


def segment_of(ends_at, token_index):
    return jnp.sum((ends_at[None, :] <= token_index[:, None]).astype(jnp.int32), axis=1)


def rotate(values, position):
    half_size = HD // 2
    inverse = 10000.0 ** (-(jnp.arange(half_size, dtype=jnp.float32) * 2.0) / HD)
    angle = position.astype(jnp.float32)[:, None, None] * inverse[None, None, :]
    cosine = jnp.cos(angle)
    sine_part = jnp.sin(angle)
    widened = values.astype(jnp.float32)
    front_half = widened[..., :half_size]
    back_half = widened[..., half_size:]
    turned = jnp.concatenate(
        [front_half * cosine - back_half * sine_part, back_half * cosine + front_half * sine_part],
        axis=-1,
    )
    return turned.astype(jnp.bfloat16)


def attention_kernel(table_ref, q_ref, lo_ref, kv_ref, *rest, has_init, finalize, per_source):
    if has_init:
        m_in, l_in, acc_in = rest[:3]
        rest = rest[3:]
    i = pl.program_id(0)
    b0 = table_ref[i * 8 + 0]
    b1 = table_ref[i * 8 + 1]
    b2 = table_ref[i * 8 + 2]
    b3 = table_ref[i * 8 + 3]
    q_first = table_ref[i * 8 + 4]
    key_offset = table_ref[i * 8 + 5]
    q = q_ref[...]
    lo = lo_ref[...]
    q_index = q_first + lax.broadcasted_iota(jnp.int32, (BQ, 1), 0)
    scale = 1.0 / math.sqrt(HD)

    def step(kb, carry, masked):
        m, l, acc = carry
        start = pl.multiple_of(kb * BK, BK)
        source = kb // per_source
        within = pl.multiple_of((kb % per_source) * BK, BK)
        keys = kv_ref[source, pl.ds(0, HD), pl.ds(within, BK)]
        vals = kv_ref[source, pl.ds(HD, HD), pl.ds(within, BK)]
        s = jnp.dot(q, keys, preferred_element_type=jnp.float32) * scale
        if masked:
            k_index = key_offset + start + lax.broadcasted_iota(jnp.int32, (1, BK), 1)
            visible = (k_index >= lo) & (k_index <= q_index)
            s = jnp.where(visible, s, NEG)
        m_new = jnp.maximum(m, jnp.max(s, axis=1, keepdims=True))
        p = jnp.exp(s - m_new)
        if masked:
            p = jnp.where(visible, p, 0.0)
        alpha = jnp.exp(m - m_new)
        l_new = l * alpha + jnp.sum(p, axis=1, keepdims=True)
        acc_new = acc * alpha + lax.dot_general(
            p.astype(jnp.bfloat16), vals, (((1,), (1,)), ((), ())), preferred_element_type=jnp.float32
        )
        return (m_new, l_new, acc_new)

    if has_init:
        carry = (m_in[...], l_in[...], acc_in[...])
    else:
        carry = (
            jnp.full((BQ, 1), NEG, jnp.float32),
            jnp.zeros((BQ, 1), jnp.float32),
            jnp.zeros((BQ, HD), jnp.float32),
        )
    carry = lax.fori_loop(b0, b1, partial(step, masked=True), carry)
    carry = lax.fori_loop(b1, b2, partial(step, masked=False), carry)
    carry = lax.fori_loop(b2, b3, partial(step, masked=True), carry)
    m, l, acc = carry
    if finalize:
        (out_ref,) = rest
        out_ref[...] = (acc / l).astype(out_ref.dtype)
    else:
        m_out, l_out, acc_out = rest
        m_out[...] = m
        l_out[...] = l
        acc_out[...] = acc


def block_table(q_first_rows, lo_first, lo_last, key_offset, key_rows):
    q_last = q_first_rows + BQ - 1
    local_lo = jnp.clip(lo_first - key_offset, 0, key_rows)
    local_hi = jnp.clip(q_last + 1 - key_offset, 0, key_rows)
    b0 = local_lo // BK
    b3 = jnp.maximum((local_hi + BK - 1) // BK, b0)
    full_lo = (jnp.maximum(lo_last - key_offset, 0) + BK - 1) // BK
    full_hi = (q_first_rows + 1 - key_offset) // BK
    b1 = jnp.clip(full_lo, b0, b3)
    b2 = jnp.clip(full_hi, b1, b3)
    offsets = jnp.broadcast_to(key_offset, q_first_rows.shape)
    zero = jnp.zeros_like(b0)
    table = jnp.stack([b0, b1, b2, b3, q_first_rows, offsets, zero, zero], axis=1)
    return table.reshape(-1).astype(jnp.int32)


def attend(table, queries, lows, kv, state, finalize, source_rows):
    rows = queries.shape[0]
    grid = (rows // BQ,)
    row_spec = lambda width: pl.BlockSpec((BQ, width), lambda i, t: (i, 0))
    in_specs = [row_spec(HD), row_spec(1), pl.BlockSpec(kv.shape, lambda i, t: (0, 0, 0))]
    operands = [queries, lows, kv]
    if state is not None:
        in_specs += [row_spec(1), row_spec(1), row_spec(HD)]
        operands += list(state)
    if finalize:
        out_shape = jax.ShapeDtypeStruct((rows, HD), jnp.bfloat16)
        out_specs = row_spec(HD)
    else:
        out_shape = (
            jax.ShapeDtypeStruct((rows, 1), jnp.float32),
            jax.ShapeDtypeStruct((rows, 1), jnp.float32),
            jax.ShapeDtypeStruct((rows, HD), jnp.float32),
        )
        out_specs = (row_spec(1), row_spec(1), row_spec(HD))
    kernel = partial(attention_kernel, has_init=state is not None, finalize=finalize, per_source=source_rows // BK)
    return pl.pallas_call(
        kernel,
        grid_spec=pltpu.PrefetchScalarGridSpec(
            num_scalar_prefetch=1,
            grid=grid,
            in_specs=in_specs,
            out_specs=out_specs,
        ),
        out_shape=out_shape,
        compiler_params=pltpu.CompilerParams(vmem_limit_bytes=48 * 1024 * 1024),
    )(table, *operands)


def per_device(lengths, page_table, projected, residual, out_weight):
    row_count = projected.shape[0]
    local_heads = projected.shape[1] // (3 * HD)
    group_size = lax.axis_size("gx")
    group_index = lax.axis_index("gx")
    first_row = group_index * row_count
    ends_at = jnp.cumsum(lengths)
    starts_at = ends_at - lengths
    own_index = first_row + jnp.arange(row_count, dtype=jnp.int32)
    own_segment = segment_of(ends_at, own_index)
    own_position = own_index - starts_at[own_segment]
    split_heads = projected.reshape(row_count, local_heads, 3, HD)
    rotated_queries = rotate(split_heads[:, :, 0], own_position)
    rotated_keys = rotate(split_heads[:, :, 1], own_position)
    key_value = jnp.concatenate([rotated_keys, split_heads[:, :, 2]], axis=-1)
    queries = rotated_queries.reshape(row_count, HD)
    local_kv = key_value.reshape(row_count, 2 * HD)
    weight_rows = out_weight.reshape(-1, 2 * HD)
    stacked_rows = row_count + weight_rows.shape[0]
    gathered = lax.all_gather(jnp.concatenate([local_kv, weight_rows], axis=0), "gx", axis=0, tiled=True)
    gathered = gathered.reshape(group_size, stacked_rows, 2 * HD)
    weight_columns = gathered[:, row_count:].reshape(-1, out_weight.shape[1])
    key_count = group_size * row_count

    lows = starts_at[own_segment]
    q_first_rows = first_row + jnp.arange(0, row_count, BQ, dtype=jnp.int32)
    lo_first = lows[0::BQ]
    lo_last = lows[BQ - 1 :: BQ]
    lows = lows.reshape(row_count, 1)
    own_table = block_table(q_first_rows, lo_first, lo_last, first_row, row_count)
    state = attend(own_table, queries, lows, local_kv.T[None], None, False, row_count)

    tail_rows = passed_along(key_value[: PAGE - 1], "gx", -1)
    extended = jnp.concatenate([key_value, tail_rows], axis=0)
    extended_index = first_row + jnp.arange(row_count + PAGE - 1, dtype=jnp.int32)
    extended_segment = jnp.minimum(segment_of(ends_at, extended_index), lengths.shape[0] - 1)
    extended_position = extended_index - starts_at[extended_segment]
    page_count = (lengths + PAGE - 1) // PAGE
    page_base = jnp.cumsum(page_count) - page_count
    logical = page_base[extended_segment] + extended_position // PAGE
    page_first = extended_index - extended_position % PAGE
    pages_held = row_count // PAGE + lengths.shape[0]
    owned = (page_first // row_count == group_index) & (extended_index < group_size * row_count)
    target = jnp.where(owned, page_table[logical] - group_index * pages_held, pages_held)
    cache_pages = jnp.zeros((pages_held, local_heads, PAGE, 2 * HD), jnp.bfloat16)
    cache_pages = cache_pages.at[target, :, extended_position % PAGE].set(extended, mode="drop")

    key_columns = jnp.swapaxes(gathered, 1, 2)
    key_columns, cache_pages, state = lax.optimization_barrier((key_columns, cache_pages, state))
    rest_table = block_table(q_first_rows, lo_first, lo_last, jnp.int32(0), jnp.minimum(first_row, key_count))
    chunk_rows = CHUNK_BLOCKS * BQ
    updates = []
    for chunk in range(row_count // chunk_rows):
        rows = slice(chunk * chunk_rows, (chunk + 1) * chunk_rows)
        table_part = rest_table[chunk * CHUNK_BLOCKS * 8 : (chunk + 1) * CHUNK_BLOCKS * 8]
        state_part = tuple(piece[rows] for piece in state)
        attended = attend(table_part, queries[rows], lows[rows], key_columns, state_part, True, row_count)
        updates.append(
            jnp.dot(
                lax.all_gather(attended, "gy", axis=1, tiled=True),
                weight_columns,
                preferred_element_type=jnp.float32,
            )
        )
    update = jnp.concatenate(updates, axis=0)
    hidden = (residual.astype(jnp.float32) + update).astype(jnp.bfloat16)
    return (hidden, cache_pages.reshape(pages_held, local_heads, PAGE * 2 * HD))


def solution(mesh):
    placed = (P(), P(), P("gx", "gy"), P("gx", "gy"), P("gx", "gy"))
    return jax.shard_map(
        per_device,
        mesh=mesh,
        in_specs=placed,
        out_specs=(P("gx", "gy"), P("gx", "gy", None)),
        check_vma=False,
    )
```

```python
from functools import partial
import math

import jax
import jax.numpy as jnp
from jax import lax
from jax.experimental import pallas as pl
from jax.experimental.pallas import tpu as pltpu
from jax.sharding import PartitionSpec as P

HD = 96
PAGE = 16
BQ = 384
BK = 768
NEG = -1e30


def passed_along(block, axis, distance):
    devices = range(lax.axis_size(axis))
    route = [(i - distance, i) for i in devices if i - distance in devices]
    return lax.ppermute(block, axis, route)


def segment_of(ends_at, token_index):
    return jnp.sum((ends_at[None, :] <= token_index[:, None]).astype(jnp.int32), axis=1)


def rotate(values, position):
    half_size = HD // 2
    inverse = 10000.0 ** (-(jnp.arange(half_size, dtype=jnp.float32) * 2.0) / HD)
    angle = position.astype(jnp.float32)[:, None, None] * inverse[None, None, :]
    cosine = jnp.cos(angle)
    sine_part = jnp.sin(angle)
    widened = values.astype(jnp.float32)
    front_half = widened[..., :half_size]
    back_half = widened[..., half_size:]
    turned = jnp.concatenate(
        [front_half * cosine - back_half * sine_part, back_half * cosine + front_half * sine_part],
        axis=-1,
    )
    return turned.astype(jnp.bfloat16)


def attention_kernel(table_ref, q_ref, lo_ref, kv_ref, *rest, has_init, finalize, per_source):
    if has_init:
        m_in, l_in, acc_in = rest[:3]
        rest = rest[3:]
    i = pl.program_id(0)
    b0 = table_ref[i * 8 + 0]
    b1 = table_ref[i * 8 + 1]
    b2 = table_ref[i * 8 + 2]
    b3 = table_ref[i * 8 + 3]
    q_first = table_ref[i * 8 + 4]
    key_offset = table_ref[i * 8 + 5]
    q = q_ref[...]
    lo = lo_ref[...]
    q_index = q_first + lax.broadcasted_iota(jnp.int32, (BQ, 1), 0)
    scale = 1.0 / math.sqrt(HD)

    def step(kb, carry, masked):
        m, l, acc = carry
        start = pl.multiple_of(kb * BK, BK)
        source = kb // per_source
        within = pl.multiple_of((kb % per_source) * BK, BK)
        keys = kv_ref[source, pl.ds(0, HD), pl.ds(within, BK)]
        vals = kv_ref[source, pl.ds(HD, HD), pl.ds(within, BK)]
        s = jnp.dot(q, keys, preferred_element_type=jnp.float32) * scale
        if masked:
            k_index = key_offset + start + lax.broadcasted_iota(jnp.int32, (1, BK), 1)
            visible = (k_index >= lo) & (k_index <= q_index)
            s = jnp.where(visible, s, NEG)
        m_new = jnp.maximum(m, jnp.max(s, axis=1, keepdims=True))
        p = jnp.exp(s - m_new)
        if masked:
            p = jnp.where(visible, p, 0.0)
        alpha = jnp.exp(m - m_new)
        l_new = l * alpha + jnp.sum(p, axis=1, keepdims=True)
        acc_new = acc * alpha + lax.dot_general(
            p.astype(jnp.bfloat16), vals, (((1,), (1,)), ((), ())), preferred_element_type=jnp.float32
        )
        return (m_new, l_new, acc_new)

    if has_init:
        carry = (m_in[...], l_in[...], acc_in[...])
    else:
        carry = (
            jnp.full((BQ, 1), NEG, jnp.float32),
            jnp.zeros((BQ, 1), jnp.float32),
            jnp.zeros((BQ, HD), jnp.float32),
        )
    carry = lax.fori_loop(b0, b1, partial(step, masked=True), carry)
    carry = lax.fori_loop(b1, b2, partial(step, masked=False), carry)
    carry = lax.fori_loop(b2, b3, partial(step, masked=True), carry)
    m, l, acc = carry
    if finalize:
        (out_ref,) = rest
        out_ref[...] = (acc / l).astype(out_ref.dtype)
    else:
        m_out, l_out, acc_out = rest
        m_out[...] = m
        l_out[...] = l
        acc_out[...] = acc


def block_table(q_first_rows, lo_first, lo_last, key_offset, key_rows):
    q_last = q_first_rows + BQ - 1
    local_lo = jnp.clip(lo_first - key_offset, 0, key_rows)
    local_hi = jnp.clip(q_last + 1 - key_offset, 0, key_rows)
    b0 = local_lo // BK
    b3 = jnp.maximum((local_hi + BK - 1) // BK, b0)
    full_lo = (jnp.maximum(lo_last - key_offset, 0) + BK - 1) // BK
    full_hi = (q_first_rows + 1 - key_offset) // BK
    b1 = jnp.clip(full_lo, b0, b3)
    b2 = jnp.clip(full_hi, b1, b3)
    offsets = jnp.broadcast_to(key_offset, q_first_rows.shape)
    zero = jnp.zeros_like(b0)
    table = jnp.stack([b0, b1, b2, b3, q_first_rows, offsets, zero, zero], axis=1)
    return table.reshape(-1).astype(jnp.int32)


def attend(table, queries, lows, kv, state, finalize, source_rows):
    rows = queries.shape[0]
    grid = (rows // BQ,)
    row_spec = lambda width: pl.BlockSpec((BQ, width), lambda i, t: (i, 0))
    in_specs = [row_spec(HD), row_spec(1), pl.BlockSpec(kv.shape, lambda i, t: (0, 0, 0))]
    operands = [queries, lows, kv]
    if state is not None:
        in_specs += [row_spec(1), row_spec(1), row_spec(HD)]
        operands += list(state)
    if finalize:
        out_shape = jax.ShapeDtypeStruct((rows, HD), jnp.bfloat16)
        out_specs = row_spec(HD)
    else:
        out_shape = (
            jax.ShapeDtypeStruct((rows, 1), jnp.float32),
            jax.ShapeDtypeStruct((rows, 1), jnp.float32),
            jax.ShapeDtypeStruct((rows, HD), jnp.float32),
        )
        out_specs = (row_spec(1), row_spec(1), row_spec(HD))
    kernel = partial(attention_kernel, has_init=state is not None, finalize=finalize, per_source=source_rows // BK)
    return pl.pallas_call(
        kernel,
        grid_spec=pltpu.PrefetchScalarGridSpec(
            num_scalar_prefetch=1,
            grid=grid,
            in_specs=in_specs,
            out_specs=out_specs,
        ),
        out_shape=out_shape,
        compiler_params=pltpu.CompilerParams(vmem_limit_bytes=48 * 1024 * 1024),
    )(table, *operands)


def per_device(lengths, page_table, projected, residual, out_weight):
    row_count = projected.shape[0]
    local_heads = projected.shape[1] // (3 * HD)
    group_size = lax.axis_size("gx")
    group_index = lax.axis_index("gx")
    first_row = group_index * row_count
    ends_at = jnp.cumsum(lengths)
    starts_at = ends_at - lengths
    own_index = first_row + jnp.arange(row_count, dtype=jnp.int32)
    own_segment = segment_of(ends_at, own_index)
    own_position = own_index - starts_at[own_segment]
    split_heads = projected.reshape(row_count, local_heads, 3, HD)
    rotated_queries = rotate(split_heads[:, :, 0], own_position)
    rotated_keys = rotate(split_heads[:, :, 1], own_position)
    key_value = jnp.concatenate([rotated_keys, split_heads[:, :, 2]], axis=-1)
    queries = rotated_queries.reshape(row_count, HD)
    local_kv = key_value.reshape(row_count, 2 * HD)
    weight_rows = out_weight.reshape(-1, 2 * HD)
    stacked_rows = row_count + weight_rows.shape[0]
    gathered = lax.all_gather(jnp.concatenate([local_kv, weight_rows], axis=0), "gx", axis=0, tiled=True)
    gathered = gathered.reshape(group_size, stacked_rows, 2 * HD)
    weight_columns = gathered[:, row_count:].reshape(-1, out_weight.shape[1])
    key_count = group_size * row_count

    half = row_count // 2
    half_blocks = half // BQ
    lows = starts_at[own_segment]
    q_first_rows = first_row + jnp.arange(0, half, BQ, dtype=jnp.int32)
    lo_first = lows[0:half:BQ]
    lo_last = lows[BQ - 1 : half : BQ]
    lows = lows.reshape(row_count, 1)
    own_table = block_table(q_first_rows, lo_first, lo_last, first_row, row_count)
    state = attend(own_table, queries[:half], lows[:half], local_kv.T[None], None, False, row_count)

    partners = [(i, group_size - 1 - i) for i in range(group_size)]
    partner_queries = lax.ppermute(queries[half:], "gx", partners)
    partner_first = (group_size - 1 - group_index) * row_count + half
    partner_index = partner_first + jnp.arange(half, dtype=jnp.int32)
    partner_lows = starts_at[segment_of(ends_at, partner_index)]
    partner_table = block_table(
        partner_first + jnp.arange(0, half, BQ, dtype=jnp.int32),
        partner_lows[0::BQ],
        partner_lows[BQ - 1 :: BQ],
        jnp.int32(0),
        key_count,
    )
    partner_lows = partner_lows.reshape(half, 1)

    tail_rows = passed_along(key_value[: PAGE - 1], "gx", -1)
    extended = jnp.concatenate([key_value, tail_rows], axis=0)
    extended_index = first_row + jnp.arange(row_count + PAGE - 1, dtype=jnp.int32)
    extended_segment = jnp.minimum(segment_of(ends_at, extended_index), lengths.shape[0] - 1)
    extended_position = extended_index - starts_at[extended_segment]
    page_count = (lengths + PAGE - 1) // PAGE
    page_base = jnp.cumsum(page_count) - page_count
    logical = page_base[extended_segment] + extended_position // PAGE
    page_first = extended_index - extended_position % PAGE
    pages_held = row_count // PAGE + lengths.shape[0]
    owned = (page_first // row_count == group_index) & (extended_index < group_size * row_count)
    target = jnp.where(owned, page_table[logical] - group_index * pages_held, pages_held)
    cache_pages = jnp.zeros((pages_held, local_heads, PAGE, 2 * HD), jnp.bfloat16)
    cache_pages = cache_pages.at[target, :, extended_position % PAGE].set(extended, mode="drop")

    key_columns = jnp.swapaxes(gathered, 1, 2)
    key_columns, cache_pages, state = lax.optimization_barrier((key_columns, cache_pages, state))
    partner_out = attend(partner_table, partner_queries, partner_lows, key_columns, None, True, row_count)
    second_half = lax.ppermute(partner_out, "gx", partners)
    rest_table = block_table(q_first_rows, lo_first, lo_last, jnp.int32(0), jnp.minimum(first_row, key_count))
    first_half = attend(rest_table, queries[:half], lows[:half], key_columns, state, True, row_count)
    updates = [
        jnp.dot(
            lax.all_gather(piece, "gy", axis=1, tiled=True),
            weight_columns,
            preferred_element_type=jnp.float32,
        )
        for piece in (first_half, second_half)
    ]
    update = jnp.concatenate(updates, axis=0)
    hidden = (residual.astype(jnp.float32) + update).astype(jnp.bfloat16)
    return (hidden, cache_pages.reshape(pages_held, local_heads, PAGE * 2 * HD))


def solution(mesh):
    placed = (P(), P(), P("gx", "gy"), P("gx", "gy"), P("gx", "gy"))
    return jax.shard_map(
        per_device,
        mesh=mesh,
        in_specs=placed,
        out_specs=(P("gx", "gy"), P("gx", "gy", None)),
        check_vma=False,
    )
```

```python
from functools import partial
import math

import jax
import jax.numpy as jnp
from jax import lax
from jax.experimental import pallas as pl
from jax.experimental.pallas import tpu as pltpu
from jax.sharding import PartitionSpec as P

HD = 96
PAGE = 16
BQ = 384
BK = 768
NEG = -1e30


def passed_along(block, axis, distance):
    devices = range(lax.axis_size(axis))
    route = [(i - distance, i) for i in devices if i - distance in devices]
    return lax.ppermute(block, axis, route)


def segment_of(ends_at, token_index):
    return jnp.sum((ends_at[None, :] <= token_index[:, None]).astype(jnp.int32), axis=1)


def rotate(values, position):
    half_size = HD // 2
    inverse = 10000.0 ** (-(jnp.arange(half_size, dtype=jnp.float32) * 2.0) / HD)
    angle = position.astype(jnp.float32)[:, None, None] * inverse[None, None, :]
    cosine = jnp.cos(angle)
    sine_part = jnp.sin(angle)
    widened = values.astype(jnp.float32)
    front_half = widened[..., :half_size]
    back_half = widened[..., half_size:]
    turned = jnp.concatenate(
        [front_half * cosine - back_half * sine_part, back_half * cosine + front_half * sine_part],
        axis=-1,
    )
    return turned.astype(jnp.bfloat16)


def attention_kernel(table_ref, q_ref, lo_ref, kv_ref, *rest, has_init, finalize, per_source):
    if has_init:
        m_in, l_in, acc_in = rest[:3]
        rest = rest[3:]
    i = pl.program_id(0)
    b0 = table_ref[i * 8 + 0]
    b1 = table_ref[i * 8 + 1]
    b2 = table_ref[i * 8 + 2]
    b3 = table_ref[i * 8 + 3]
    q_first = table_ref[i * 8 + 4]
    key_offset = table_ref[i * 8 + 5]
    q = q_ref[...]
    lo = lo_ref[...]
    q_index = q_first + lax.broadcasted_iota(jnp.int32, (BQ, 1), 0)
    scale = 1.0 / math.sqrt(HD)

    def step(kb, carry, masked):
        m, l, acc = carry
        start = pl.multiple_of(kb * BK, BK)
        source = kb // per_source
        within = pl.multiple_of((kb % per_source) * BK, BK)
        keys = kv_ref[source, pl.ds(0, HD), pl.ds(within, BK)]
        vals = kv_ref[source, pl.ds(HD, HD), pl.ds(within, BK)]
        s = jnp.dot(q, keys, preferred_element_type=jnp.float32) * scale
        if masked:
            k_index = key_offset + start + lax.broadcasted_iota(jnp.int32, (1, BK), 1)
            visible = (k_index >= lo) & (k_index <= q_index)
            s = jnp.where(visible, s, NEG)
        m_new = jnp.maximum(m, jnp.max(s, axis=1, keepdims=True))
        p = jnp.exp(s - m_new)
        if masked:
            p = jnp.where(visible, p, 0.0)
        alpha = jnp.exp(m - m_new)
        l_new = l * alpha + jnp.sum(p, axis=1, keepdims=True)
        acc_new = acc * alpha + lax.dot_general(
            p.astype(jnp.bfloat16), vals, (((1,), (1,)), ((), ())), preferred_element_type=jnp.float32
        )
        return (m_new, l_new, acc_new)

    if has_init:
        carry = (m_in[...], l_in[...], acc_in[...])
    else:
        carry = (
            jnp.full((BQ, 1), NEG, jnp.float32),
            jnp.zeros((BQ, 1), jnp.float32),
            jnp.zeros((BQ, HD), jnp.float32),
        )
    carry = lax.fori_loop(b0, b1, partial(step, masked=True), carry)
    carry = lax.fori_loop(b1, b2, partial(step, masked=False), carry)
    carry = lax.fori_loop(b2, b3, partial(step, masked=True), carry)
    m, l, acc = carry
    if finalize:
        (out_ref,) = rest
        out_ref[...] = (acc / l).astype(out_ref.dtype)
    else:
        m_out, l_out, acc_out = rest
        m_out[...] = m
        l_out[...] = l
        acc_out[...] = acc


def block_table(q_first_rows, lo_first, lo_last, key_offset, key_rows):
    q_last = q_first_rows + BQ - 1
    local_lo = jnp.clip(lo_first - key_offset, 0, key_rows)
    local_hi = jnp.clip(q_last + 1 - key_offset, 0, key_rows)
    b0 = local_lo // BK
    b3 = jnp.maximum((local_hi + BK - 1) // BK, b0)
    full_lo = (jnp.maximum(lo_last - key_offset, 0) + BK - 1) // BK
    full_hi = (q_first_rows + 1 - key_offset) // BK
    b1 = jnp.clip(full_lo, b0, b3)
    b2 = jnp.clip(full_hi, b1, b3)
    offsets = jnp.broadcast_to(key_offset, q_first_rows.shape)
    zero = jnp.zeros_like(b0)
    table = jnp.stack([b0, b1, b2, b3, q_first_rows, offsets, zero, zero], axis=1)
    return table.reshape(-1).astype(jnp.int32)


def attend(table, queries, lows, kv, state, finalize, source_rows):
    rows = queries.shape[0]
    grid = (rows // BQ,)
    row_spec = lambda width: pl.BlockSpec((BQ, width), lambda i, t: (i, 0))
    in_specs = [row_spec(HD), row_spec(1), pl.BlockSpec(kv.shape, lambda i, t: (0, 0, 0))]
    operands = [queries, lows, kv]
    if state is not None:
        in_specs += [row_spec(1), row_spec(1), row_spec(HD)]
        operands += list(state)
    if finalize:
        out_shape = jax.ShapeDtypeStruct((rows, HD), jnp.bfloat16)
        out_specs = row_spec(HD)
    else:
        out_shape = (
            jax.ShapeDtypeStruct((rows, 1), jnp.float32),
            jax.ShapeDtypeStruct((rows, 1), jnp.float32),
            jax.ShapeDtypeStruct((rows, HD), jnp.float32),
        )
        out_specs = (row_spec(1), row_spec(1), row_spec(HD))
    kernel = partial(attention_kernel, has_init=state is not None, finalize=finalize, per_source=source_rows // BK)
    return pl.pallas_call(
        kernel,
        grid_spec=pltpu.PrefetchScalarGridSpec(
            num_scalar_prefetch=1,
            grid=grid,
            in_specs=in_specs,
            out_specs=out_specs,
        ),
        out_shape=out_shape,
        compiler_params=pltpu.CompilerParams(vmem_limit_bytes=48 * 1024 * 1024),
    )(table, *operands)


def per_device(lengths, page_table, projected, residual, out_weight):
    row_count = projected.shape[0]
    local_heads = projected.shape[1] // (3 * HD)
    group_size = lax.axis_size("gx")
    group_index = lax.axis_index("gx")
    first_row = group_index * row_count
    ends_at = jnp.cumsum(lengths)
    starts_at = ends_at - lengths
    own_index = first_row + jnp.arange(row_count, dtype=jnp.int32)
    own_segment = segment_of(ends_at, own_index)
    own_position = own_index - starts_at[own_segment]
    split_heads = projected.reshape(row_count, local_heads, 3, HD)
    rotated_queries = rotate(split_heads[:, :, 0], own_position)
    rotated_keys = rotate(split_heads[:, :, 1], own_position)
    key_value = jnp.concatenate([rotated_keys, split_heads[:, :, 2]], axis=-1)
    queries = rotated_queries.reshape(row_count, HD)
    local_kv = key_value.reshape(row_count, 2 * HD)
    weight_rows = out_weight.reshape(-1, 2 * HD)
    stacked_rows = row_count + weight_rows.shape[0]
    gathered = lax.all_gather(jnp.concatenate([local_kv, weight_rows], axis=0), "gx", axis=0, tiled=True)
    gathered = gathered.reshape(group_size, stacked_rows, 2 * HD)
    weight_columns = gathered[:, row_count:].reshape(-1, out_weight.shape[1])
    key_count = group_size * row_count

    half = row_count // 2
    half_blocks = half // BQ
    lows = starts_at[own_segment]
    q_first_rows = first_row + jnp.arange(0, half, BQ, dtype=jnp.int32)
    lo_first = lows[0:half:BQ]
    lo_last = lows[BQ - 1 : half : BQ]
    lows = lows.reshape(row_count, 1)
    own_table = block_table(q_first_rows, lo_first, lo_last, first_row, row_count)
    state = attend(own_table, queries[:half], lows[:half], local_kv.T[None], None, False, row_count)

    partners = [(i, group_size - 1 - i) for i in range(group_size)]
    partner_queries = lax.ppermute(queries[half:], "gx", partners)
    partner_residual = lax.ppermute(residual[half:], "gx", partners)
    partner_first = (group_size - 1 - group_index) * row_count + half
    partner_index = partner_first + jnp.arange(half, dtype=jnp.int32)
    partner_lows = starts_at[segment_of(ends_at, partner_index)]
    partner_table = block_table(
        partner_first + jnp.arange(0, half, BQ, dtype=jnp.int32),
        partner_lows[0::BQ],
        partner_lows[BQ - 1 :: BQ],
        jnp.int32(0),
        key_count,
    )
    partner_lows = partner_lows.reshape(half, 1)

    tail_rows = passed_along(key_value[: PAGE - 1], "gx", -1)
    extended = jnp.concatenate([key_value, tail_rows], axis=0)
    extended_index = first_row + jnp.arange(row_count + PAGE - 1, dtype=jnp.int32)
    extended_segment = jnp.minimum(segment_of(ends_at, extended_index), lengths.shape[0] - 1)
    extended_position = extended_index - starts_at[extended_segment]
    page_count = (lengths + PAGE - 1) // PAGE
    page_base = jnp.cumsum(page_count) - page_count
    logical = page_base[extended_segment] + extended_position // PAGE
    page_first = extended_index - extended_position % PAGE
    pages_held = row_count // PAGE + lengths.shape[0]
    owned = (page_first // row_count == group_index) & (extended_index < group_size * row_count)
    target = jnp.where(owned, page_table[logical] - group_index * pages_held, pages_held)
    cache_pages = jnp.zeros((pages_held, local_heads, PAGE, 2 * HD), jnp.bfloat16)
    cache_pages = cache_pages.at[target, :, extended_position % PAGE].set(extended, mode="drop")

    key_columns = jnp.swapaxes(gathered, 1, 2)
    key_columns, cache_pages, state, partner_queries, partner_residual = lax.optimization_barrier(
        (key_columns, cache_pages, state, partner_queries, partner_residual)
    )
    rest_table = block_table(q_first_rows, lo_first, lo_last, jnp.int32(0), jnp.minimum(first_row, key_count))
    first_half = attend(rest_table, queries[:half], lows[:half], key_columns, state, True, row_count)
    partner_out = attend(partner_table, partner_queries, partner_lows, key_columns, None, True, row_count)

    def projected_rows(piece, rows_residual):
        update = jnp.dot(
            lax.all_gather(piece, "gy", axis=1, tiled=True),
            weight_columns,
            preferred_element_type=jnp.float32,
        )
        return (rows_residual.astype(jnp.float32) + update).astype(jnp.bfloat16)

    hidden_first = projected_rows(first_half, residual[:half])
    hidden_second = lax.ppermute(projected_rows(partner_out, partner_residual), "gx", partners)
    hidden = jnp.concatenate([hidden_first, hidden_second], axis=0)
    return (hidden, cache_pages.reshape(pages_held, local_heads, PAGE * 2 * HD))


def solution(mesh):
    placed = (P(), P(), P("gx", "gy"), P("gx", "gy"), P("gx", "gy"))
    return jax.shard_map(
        per_device,
        mesh=mesh,
        in_specs=placed,
        out_specs=(P("gx", "gy"), P("gx", "gy", None)),
        check_vma=False,
    )
```

```python
from functools import partial
import math

import jax
import jax.numpy as jnp
from jax import lax
from jax.experimental import pallas as pl
from jax.experimental.pallas import tpu as pltpu
from jax.sharding import PartitionSpec as P

HD = 96
PAGE = 16
BQ = 384
BK = 768
NEG = -1e30


def passed_along(block, axis, distance):
    devices = range(lax.axis_size(axis))
    route = [(i - distance, i) for i in devices if i - distance in devices]
    return lax.ppermute(block, axis, route)


def segment_of(ends_at, token_index):
    return jnp.sum((ends_at[None, :] <= token_index[:, None]).astype(jnp.int32), axis=1)


def rotate(values, position):
    half_size = HD // 2
    inverse = 10000.0 ** (-(jnp.arange(half_size, dtype=jnp.float32) * 2.0) / HD)
    angle = position.astype(jnp.float32)[:, None, None] * inverse[None, None, :]
    cosine = jnp.cos(angle)
    sine_part = jnp.sin(angle)
    widened = values.astype(jnp.float32)
    front_half = widened[..., :half_size]
    back_half = widened[..., half_size:]
    turned = jnp.concatenate(
        [front_half * cosine - back_half * sine_part, back_half * cosine + front_half * sine_part],
        axis=-1,
    )
    return turned.astype(jnp.bfloat16)


def attention_kernel(table_ref, q_ref, lo_ref, kv_ref, *rest, has_init, finalize, per_source):
    if has_init:
        m_in, l_in, acc_in = rest[:3]
        rest = rest[3:]
    i = pl.program_id(0)
    b0 = table_ref[i * 8 + 0]
    b1 = table_ref[i * 8 + 1]
    b2 = table_ref[i * 8 + 2]
    b3 = table_ref[i * 8 + 3]
    q_first = table_ref[i * 8 + 4]
    key_offset = table_ref[i * 8 + 5]
    q = q_ref[...]
    lo = lo_ref[...]
    q_index = q_first + lax.broadcasted_iota(jnp.int32, (BQ, 1), 0)
    scale = 1.0 / math.sqrt(HD)

    def step(kb, carry, masked):
        m, l, acc = carry
        start = pl.multiple_of(kb * BK, BK)
        source = kb // per_source
        within = pl.multiple_of((kb % per_source) * BK, BK)
        keys = kv_ref[source, pl.ds(0, HD), pl.ds(within, BK)]
        vals = kv_ref[source, pl.ds(HD, HD), pl.ds(within, BK)]
        s = jnp.dot(q, keys, preferred_element_type=jnp.float32) * scale
        if masked:
            k_index = key_offset + start + lax.broadcasted_iota(jnp.int32, (1, BK), 1)
            visible = (k_index >= lo) & (k_index <= q_index)
            s = jnp.where(visible, s, NEG)
        m_new = jnp.maximum(m, jnp.max(s, axis=1, keepdims=True))
        p = jnp.exp(s - m_new)
        if masked:
            p = jnp.where(visible, p, 0.0)
        alpha = jnp.exp(m - m_new)
        l_new = l * alpha + jnp.sum(p, axis=1, keepdims=True)
        acc_new = acc * alpha + lax.dot_general(
            p.astype(jnp.bfloat16), vals, (((1,), (1,)), ((), ())), preferred_element_type=jnp.float32
        )
        return (m_new, l_new, acc_new)

    if has_init:
        carry = (m_in[...], l_in[...], acc_in[...])
    else:
        carry = (
            jnp.full((BQ, 1), NEG, jnp.float32),
            jnp.zeros((BQ, 1), jnp.float32),
            jnp.zeros((BQ, HD), jnp.float32),
        )
    carry = lax.fori_loop(b0, b1, partial(step, masked=True), carry)
    carry = lax.fori_loop(b1, b2, partial(step, masked=False), carry)
    carry = lax.fori_loop(b2, b3, partial(step, masked=True), carry)
    m, l, acc = carry
    if finalize:
        (out_ref,) = rest
        out_ref[...] = (acc / l).astype(out_ref.dtype)
    else:
        m_out, l_out, acc_out = rest
        m_out[...] = m
        l_out[...] = l
        acc_out[...] = acc


def block_table(q_first_rows, lo_first, lo_last, key_offset, key_rows):
    q_last = q_first_rows + BQ - 1
    local_lo = jnp.clip(lo_first - key_offset, 0, key_rows)
    local_hi = jnp.clip(q_last + 1 - key_offset, 0, key_rows)
    b0 = local_lo // BK
    b3 = jnp.maximum((local_hi + BK - 1) // BK, b0)
    full_lo = (jnp.maximum(lo_last - key_offset, 0) + BK - 1) // BK
    full_hi = (q_first_rows + 1 - key_offset) // BK
    b1 = jnp.clip(full_lo, b0, b3)
    b2 = jnp.clip(full_hi, b1, b3)
    offsets = jnp.broadcast_to(key_offset, q_first_rows.shape)
    zero = jnp.zeros_like(b0)
    table = jnp.stack([b0, b1, b2, b3, q_first_rows, offsets, zero, zero], axis=1)
    return table.reshape(-1).astype(jnp.int32)


def attend(table, queries, lows, kv, state, finalize, source_rows):
    rows = queries.shape[0]
    grid = (rows // BQ,)
    row_spec = lambda width: pl.BlockSpec((BQ, width), lambda i, t: (i, 0))
    in_specs = [row_spec(HD), row_spec(1), pl.BlockSpec(kv.shape, lambda i, t: (0, 0, 0))]
    operands = [queries, lows, kv]
    if state is not None:
        in_specs += [row_spec(1), row_spec(1), row_spec(HD)]
        operands += list(state)
    if finalize:
        out_shape = jax.ShapeDtypeStruct((rows, HD), jnp.bfloat16)
        out_specs = row_spec(HD)
    else:
        out_shape = (
            jax.ShapeDtypeStruct((rows, 1), jnp.float32),
            jax.ShapeDtypeStruct((rows, 1), jnp.float32),
            jax.ShapeDtypeStruct((rows, HD), jnp.float32),
        )
        out_specs = (row_spec(1), row_spec(1), row_spec(HD))
    kernel = partial(attention_kernel, has_init=state is not None, finalize=finalize, per_source=source_rows // BK)
    return pl.pallas_call(
        kernel,
        grid_spec=pltpu.PrefetchScalarGridSpec(
            num_scalar_prefetch=1,
            grid=grid,
            in_specs=in_specs,
            out_specs=out_specs,
        ),
        out_shape=out_shape,
        compiler_params=pltpu.CompilerParams(vmem_limit_bytes=48 * 1024 * 1024),
    )(table, *operands)


def per_device(lengths, page_table, projected, residual, out_weight):
    row_count = projected.shape[0]
    local_heads = projected.shape[1] // (3 * HD)
    group_size = lax.axis_size("gx")
    group_index = lax.axis_index("gx")
    first_row = group_index * row_count
    ends_at = jnp.cumsum(lengths)
    starts_at = ends_at - lengths
    own_index = first_row + jnp.arange(row_count, dtype=jnp.int32)
    own_segment = segment_of(ends_at, own_index)
    own_position = own_index - starts_at[own_segment]
    split_heads = projected.reshape(row_count, local_heads, 3, HD)
    rotated_queries = rotate(split_heads[:, :, 0], own_position)
    rotated_keys = rotate(split_heads[:, :, 1], own_position)
    key_value = jnp.concatenate([rotated_keys, split_heads[:, :, 2]], axis=-1)
    queries = rotated_queries.reshape(row_count, HD)
    local_kv = key_value.reshape(row_count, 2 * HD)
    weight_rows = out_weight.reshape(-1, 2 * HD)
    stacked_rows = row_count + weight_rows.shape[0]
    gathered = lax.all_gather(jnp.concatenate([local_kv, weight_rows], axis=0), "gx", axis=0, tiled=True)
    gathered = gathered.reshape(group_size, stacked_rows, 2 * HD)
    weight_columns = gathered[:, row_count:].reshape(-1, out_weight.shape[1])
    key_count = group_size * row_count

    half = row_count // 2
    half_blocks = half // BQ
    lows = starts_at[own_segment]
    q_first_rows = first_row + jnp.arange(0, half, BQ, dtype=jnp.int32)
    lo_first = lows[0:half:BQ]
    lo_last = lows[BQ - 1 : half : BQ]
    lows = lows.reshape(row_count, 1)
    own_table = block_table(q_first_rows, lo_first, lo_last, first_row, row_count)
    state = attend(own_table, queries[:half], lows[:half], local_kv.T[None], None, False, row_count)

    partners = [(i, group_size - 1 - i) for i in range(group_size)]
    partner_queries = lax.ppermute(queries[half:], "gx", partners)
    partner_residual = lax.ppermute(residual[half:], "gx", partners)
    partner_first = (group_size - 1 - group_index) * row_count + half
    partner_index = partner_first + jnp.arange(half, dtype=jnp.int32)
    partner_lows = starts_at[segment_of(ends_at, partner_index)]
    partner_table = block_table(
        partner_first + jnp.arange(0, half, BQ, dtype=jnp.int32),
        partner_lows[0::BQ],
        partner_lows[BQ - 1 :: BQ],
        jnp.int32(0),
        key_count,
    )
    partner_lows = partner_lows.reshape(half, 1)

    tail_rows = passed_along(key_value[: PAGE - 1], "gx", -1)
    extended = jnp.concatenate([key_value, tail_rows], axis=0)
    extended_index = first_row + jnp.arange(row_count + PAGE - 1, dtype=jnp.int32)
    extended_segment = jnp.minimum(segment_of(ends_at, extended_index), lengths.shape[0] - 1)
    extended_position = extended_index - starts_at[extended_segment]
    page_count = (lengths + PAGE - 1) // PAGE
    page_base = jnp.cumsum(page_count) - page_count
    logical = page_base[extended_segment] + extended_position // PAGE
    page_first = extended_index - extended_position % PAGE
    pages_held = row_count // PAGE + lengths.shape[0]
    owned = (page_first // row_count == group_index) & (extended_index < group_size * row_count)
    target = jnp.where(owned, page_table[logical] - group_index * pages_held, pages_held)
    cache_pages = jnp.zeros((pages_held, local_heads, PAGE, 2 * HD), jnp.bfloat16)
    cache_pages = cache_pages.at[target, :, extended_position % PAGE].set(extended, mode="drop")

    key_columns = jnp.swapaxes(gathered, 1, 2)
    key_columns, cache_pages, state, partner_queries, partner_residual = lax.optimization_barrier(
        (key_columns, cache_pages, state, partner_queries, partner_residual)
    )
    rest_table = block_table(q_first_rows, lo_first, lo_last, jnp.int32(0), jnp.minimum(first_row, key_count))
    first_half = attend(rest_table, queries[:half], lows[:half], key_columns, state, True, row_count)
    partner_out = attend(partner_table, partner_queries, partner_lows, key_columns, None, True, row_count)

    core = lax.axis_index("core")
    pair_weights = lax.all_gather(weight_columns, "core", axis=1, tiled=True)

    def projected_rows(piece, rows_residual):
        pair = lax.all_gather(piece, "core", axis=1, tiled=True)
        share = pair.shape[0] // 2
        mine = lax.dynamic_slice_in_dim(pair, core * share, share, axis=0)
        update = jnp.dot(
            lax.all_gather(mine, "gc", axis=1, tiled=True),
            pair_weights,
            preferred_element_type=jnp.float32,
        )
        update = lax.all_to_all(update, "core", 1, 0, tiled=True)
        return (rows_residual.astype(jnp.float32) + update).astype(jnp.bfloat16)

    hidden_first = projected_rows(first_half, residual[:half])
    hidden_second = lax.ppermute(projected_rows(partner_out, partner_residual), "gx", partners)
    hidden = jnp.concatenate([hidden_first, hidden_second], axis=0)
    return (hidden, cache_pages.reshape(pages_held, local_heads, PAGE * 2 * HD))


def solution(mesh):
    chips = mesh.devices.reshape(mesh.devices.shape[0], -1, 2)
    paired = jax.sharding.Mesh(chips, ("gx", "gc", "core"))
    tokens_heads = P("gx", ("gc", "core"))
    placed = (P(), P(), tokens_heads, tokens_heads, tokens_heads)
    return jax.shard_map(
        per_device,
        mesh=paired,
        in_specs=placed,
        out_specs=(tokens_heads, P("gx", ("gc", "core"), None)),
        check_vma=False,
    )
```

```python
from functools import partial
import math

import jax
import jax.numpy as jnp
from jax import lax
from jax.experimental import pallas as pl
from jax.experimental.pallas import tpu as pltpu
from jax.sharding import PartitionSpec as P

HD = 96
PAGE = 16
BQ = 384
BK = 768
NEG = -1e30


def passed_along(block, axis, distance):
    devices = range(lax.axis_size(axis))
    route = [(i - distance, i) for i in devices if i - distance in devices]
    return lax.ppermute(block, axis, route)


def segment_of(ends_at, token_index):
    return jnp.sum((ends_at[None, :] <= token_index[:, None]).astype(jnp.int32), axis=1)


def rotate(values, position):
    half_size = HD // 2
    inverse = 10000.0 ** (-(jnp.arange(half_size, dtype=jnp.float32) * 2.0) / HD)
    angle = position.astype(jnp.float32)[:, None, None] * inverse[None, None, :]
    cosine = jnp.cos(angle)
    sine_part = jnp.sin(angle)
    widened = values.astype(jnp.float32)
    front_half = widened[..., :half_size]
    back_half = widened[..., half_size:]
    turned = jnp.concatenate(
        [front_half * cosine - back_half * sine_part, back_half * cosine + front_half * sine_part],
        axis=-1,
    )
    return turned.astype(jnp.bfloat16)


def attention_kernel(table_ref, q_ref, lo_ref, kv_ref, *rest, has_init, finalize, per_source):
    if has_init:
        m_in, l_in, acc_in = rest[:3]
        rest = rest[3:]
    i = pl.program_id(0)
    b0 = table_ref[i * 8 + 0]
    b1 = table_ref[i * 8 + 1]
    b2 = table_ref[i * 8 + 2]
    b3 = table_ref[i * 8 + 3]
    q_first = table_ref[i * 8 + 4]
    key_offset = table_ref[i * 8 + 5]
    q = q_ref[...]
    lo = lo_ref[...]
    q_index = q_first + lax.broadcasted_iota(jnp.int32, (BQ, 1), 0)
    scale = 1.0 / math.sqrt(HD)

    def step(kb, carry, masked):
        m, l, acc = carry
        start = pl.multiple_of(kb * BK, BK)
        source = kb // per_source
        within = pl.multiple_of((kb % per_source) * BK, BK)
        keys = kv_ref[source, pl.ds(0, HD), pl.ds(within, BK)]
        vals = kv_ref[source, pl.ds(HD, HD), pl.ds(within, BK)]
        s = jnp.dot(q, keys, preferred_element_type=jnp.float32) * scale
        if masked:
            k_index = key_offset + start + lax.broadcasted_iota(jnp.int32, (1, BK), 1)
            visible = (k_index >= lo) & (k_index <= q_index)
            s = jnp.where(visible, s, NEG)
        m_new = jnp.maximum(m, jnp.max(s, axis=1, keepdims=True))
        p = jnp.exp(s - m_new)
        if masked:
            p = jnp.where(visible, p, 0.0)
        alpha = jnp.exp(m - m_new)
        l_new = l * alpha + jnp.sum(p, axis=1, keepdims=True)
        acc_new = acc * alpha + lax.dot_general(
            p.astype(jnp.bfloat16), vals, (((1,), (1,)), ((), ())), preferred_element_type=jnp.float32
        )
        return (m_new, l_new, acc_new)

    if has_init:
        carry = (m_in[...], l_in[...], acc_in[...])
    else:
        carry = (
            jnp.full((BQ, 1), NEG, jnp.float32),
            jnp.zeros((BQ, 1), jnp.float32),
            jnp.zeros((BQ, HD), jnp.float32),
        )
    carry = lax.fori_loop(b0, b1, partial(step, masked=True), carry)
    carry = lax.fori_loop(b1, b2, partial(step, masked=False), carry)
    carry = lax.fori_loop(b2, b3, partial(step, masked=True), carry)
    m, l, acc = carry
    if finalize:
        (out_ref,) = rest
        out_ref[...] = (acc / l).astype(out_ref.dtype)
    else:
        m_out, l_out, acc_out = rest
        m_out[...] = m
        l_out[...] = l
        acc_out[...] = acc


def block_table(q_first_rows, lo_first, lo_last, key_offset, key_rows):
    q_last = q_first_rows + BQ - 1
    local_lo = jnp.clip(lo_first - key_offset, 0, key_rows)
    local_hi = jnp.clip(q_last + 1 - key_offset, 0, key_rows)
    b0 = local_lo // BK
    b3 = jnp.maximum((local_hi + BK - 1) // BK, b0)
    full_lo = (jnp.maximum(lo_last - key_offset, 0) + BK - 1) // BK
    full_hi = (q_first_rows + 1 - key_offset) // BK
    b1 = jnp.clip(full_lo, b0, b3)
    b2 = jnp.clip(full_hi, b1, b3)
    offsets = jnp.broadcast_to(key_offset, q_first_rows.shape)
    zero = jnp.zeros_like(b0)
    table = jnp.stack([b0, b1, b2, b3, q_first_rows, offsets, zero, zero], axis=1)
    return table.reshape(-1).astype(jnp.int32)


def attend(table, queries, lows, kv, state, finalize, source_rows):
    rows = queries.shape[0]
    grid = (rows // BQ,)
    row_spec = lambda width: pl.BlockSpec((BQ, width), lambda i, t: (i, 0))
    in_specs = [row_spec(HD), row_spec(1), pl.BlockSpec(kv.shape, lambda i, t: (0, 0, 0))]
    operands = [queries, lows, kv]
    if state is not None:
        in_specs += [row_spec(1), row_spec(1), row_spec(HD)]
        operands += list(state)
    if finalize:
        out_shape = jax.ShapeDtypeStruct((rows, HD), jnp.bfloat16)
        out_specs = row_spec(HD)
    else:
        out_shape = (
            jax.ShapeDtypeStruct((rows, 1), jnp.float32),
            jax.ShapeDtypeStruct((rows, 1), jnp.float32),
            jax.ShapeDtypeStruct((rows, HD), jnp.float32),
        )
        out_specs = (row_spec(1), row_spec(1), row_spec(HD))
    kernel = partial(attention_kernel, has_init=state is not None, finalize=finalize, per_source=source_rows // BK)
    return pl.pallas_call(
        kernel,
        grid_spec=pltpu.PrefetchScalarGridSpec(
            num_scalar_prefetch=1,
            grid=grid,
            in_specs=in_specs,
            out_specs=out_specs,
        ),
        out_shape=out_shape,
        compiler_params=pltpu.CompilerParams(vmem_limit_bytes=48 * 1024 * 1024),
    )(table, *operands)


def per_device(lengths, page_table, projected, residual, out_weight):
    row_count = projected.shape[0]
    local_heads = projected.shape[1] // (3 * HD)
    group_size = lax.axis_size("gx")
    group_index = lax.axis_index("gx")
    first_row = group_index * row_count
    ends_at = jnp.cumsum(lengths)
    starts_at = ends_at - lengths
    own_index = first_row + jnp.arange(row_count, dtype=jnp.int32)
    own_segment = segment_of(ends_at, own_index)
    own_position = own_index - starts_at[own_segment]
    split_heads = projected.reshape(row_count, local_heads, 3, HD)
    rotated_queries = rotate(split_heads[:, :, 0], own_position)
    rotated_keys = rotate(split_heads[:, :, 1], own_position)
    key_value = jnp.concatenate([rotated_keys, split_heads[:, :, 2]], axis=-1)
    queries = rotated_queries.reshape(row_count, HD)
    local_kv = key_value.reshape(row_count, 2 * HD)
    weight_rows = out_weight.reshape(-1, 2 * HD)
    stacked_rows = row_count + weight_rows.shape[0]
    gathered = lax.all_gather(jnp.concatenate([local_kv, weight_rows], axis=0), "gx", axis=0, tiled=True)
    gathered = gathered.reshape(group_size, stacked_rows, 2 * HD)
    weight_columns = gathered[:, row_count:].reshape(-1, out_weight.shape[1])
    key_count = group_size * row_count

    half = row_count // 2
    half_blocks = half // BQ
    lows = starts_at[own_segment]
    q_first_rows = first_row + jnp.arange(0, half, BQ, dtype=jnp.int32)
    lo_first = lows[0:half:BQ]
    lo_last = lows[BQ - 1 : half : BQ]
    lows = lows.reshape(row_count, 1)
    own_table = block_table(q_first_rows, lo_first, lo_last, first_row, row_count)
    state = attend(own_table, queries[:half], lows[:half], local_kv.T[None], None, False, row_count)

    partners = [(i, group_size - 1 - i) for i in range(group_size)]
    partner_queries = lax.ppermute(queries[half:], "gx", partners)
    partner_residual = lax.ppermute(residual[half:], "gx", partners)
    partner_first = (group_size - 1 - group_index) * row_count + half
    partner_index = partner_first + jnp.arange(half, dtype=jnp.int32)
    partner_lows = starts_at[segment_of(ends_at, partner_index)]
    partner_table = block_table(
        partner_first + jnp.arange(0, half, BQ, dtype=jnp.int32),
        partner_lows[0::BQ],
        partner_lows[BQ - 1 :: BQ],
        jnp.int32(0),
        key_count,
    )
    partner_lows = partner_lows.reshape(half, 1)

    tail_rows = passed_along(key_value[: PAGE - 1], "gx", -1)
    extended = jnp.concatenate([key_value, tail_rows], axis=0)
    extended_index = first_row + jnp.arange(row_count + PAGE - 1, dtype=jnp.int32)
    extended_segment = jnp.minimum(segment_of(ends_at, extended_index), lengths.shape[0] - 1)
    extended_position = extended_index - starts_at[extended_segment]
    page_count = (lengths + PAGE - 1) // PAGE
    page_base = jnp.cumsum(page_count) - page_count
    logical = page_base[extended_segment] + extended_position // PAGE
    page_first = extended_index - extended_position % PAGE
    pages_held = row_count // PAGE + lengths.shape[0]
    owned = (page_first // row_count == group_index) & (extended_index < group_size * row_count)
    target = jnp.where(owned, page_table[logical] - group_index * pages_held, pages_held)
    cache_pages = jnp.zeros((pages_held, local_heads, PAGE, 2 * HD), jnp.bfloat16)
    cache_pages = cache_pages.at[target, :, extended_position % PAGE].set(extended, mode="drop")

    key_columns = jnp.swapaxes(gathered, 1, 2)
    key_columns, cache_pages, state, partner_queries, partner_residual = lax.optimization_barrier(
        (key_columns, cache_pages, state, partner_queries, partner_residual)
    )
    rest_table = block_table(q_first_rows, lo_first, lo_last, jnp.int32(0), jnp.minimum(first_row, key_count))
    first_half = attend(rest_table, queries[:half], lows[:half], key_columns, state, True, row_count)
    partner_out = attend(partner_table, partner_queries, partner_lows, key_columns, None, True, row_count)

    both = jnp.concatenate([first_half, partner_out], axis=0)
    update = jnp.dot(
        lax.all_gather(both, "gy", axis=1, tiled=True),
        weight_columns,
        preferred_element_type=jnp.float32,
    )
    both_residual = jnp.concatenate([residual[:half], partner_residual], axis=0)
    projected = (both_residual.astype(jnp.float32) + update).astype(jnp.bfloat16)
    hidden_second = lax.ppermute(projected[half:], "gx", partners)
    hidden = jnp.concatenate([projected[:half], hidden_second], axis=0)
    return (hidden, cache_pages.reshape(pages_held, local_heads, PAGE * 2 * HD))


def solution(mesh):
    placed = (P(), P(), P("gx", "gy"), P("gx", "gy"), P("gx", "gy"))
    return jax.shard_map(
        per_device,
        mesh=mesh,
        in_specs=placed,
        out_specs=(P("gx", "gy"), P("gx", "gy", None)),
        check_vma=False,
    )
```

```python
from functools import partial
import math

import jax
import jax.numpy as jnp
from jax import lax
from jax.experimental import pallas as pl
from jax.experimental.pallas import tpu as pltpu
from jax.sharding import PartitionSpec as P

HD = 96
PAGE = 16
BQ = 384
BK = 1152
NEG = -1e30


def passed_along(block, axis, distance):
    devices = range(lax.axis_size(axis))
    route = [(i - distance, i) for i in devices if i - distance in devices]
    return lax.ppermute(block, axis, route)


def segment_of(ends_at, token_index):
    return jnp.sum((ends_at[None, :] <= token_index[:, None]).astype(jnp.int32), axis=1)


def rotate(values, position):
    half_size = HD // 2
    inverse = 10000.0 ** (-(jnp.arange(half_size, dtype=jnp.float32) * 2.0) / HD)
    angle = position.astype(jnp.float32)[:, None, None] * inverse[None, None, :]
    cosine = jnp.cos(angle)
    sine_part = jnp.sin(angle)
    widened = values.astype(jnp.float32)
    front_half = widened[..., :half_size]
    back_half = widened[..., half_size:]
    turned = jnp.concatenate(
        [front_half * cosine - back_half * sine_part, back_half * cosine + front_half * sine_part],
        axis=-1,
    )
    return turned.astype(jnp.bfloat16)


def attention_kernel(table_ref, q_ref, lo_ref, kv_ref, *rest, has_init, finalize, per_source):
    if has_init:
        m_in, l_in, acc_in = rest[:3]
        rest = rest[3:]
    i = pl.program_id(0)
    b0 = table_ref[i * 8 + 0]
    b1 = table_ref[i * 8 + 1]
    b2 = table_ref[i * 8 + 2]
    b3 = table_ref[i * 8 + 3]
    q_first = table_ref[i * 8 + 4]
    key_offset = table_ref[i * 8 + 5]
    q = q_ref[...]
    lo = lo_ref[...]
    q_index = q_first + lax.broadcasted_iota(jnp.int32, (BQ, 1), 0)
    scale = 1.0 / math.sqrt(HD)

    def step(kb, carry, masked):
        m, l, acc = carry
        start = pl.multiple_of(kb * BK, BK)
        source = kb // per_source
        within = pl.multiple_of((kb % per_source) * BK, BK)
        keys = kv_ref[source, pl.ds(0, HD), pl.ds(within, BK)]
        vals = kv_ref[source, pl.ds(HD, HD), pl.ds(within, BK)]
        s = jnp.dot(q, keys, preferred_element_type=jnp.float32) * scale
        if masked:
            k_index = key_offset + start + lax.broadcasted_iota(jnp.int32, (1, BK), 1)
            visible = (k_index >= lo) & (k_index <= q_index)
            s = jnp.where(visible, s, NEG)
        m_new = jnp.maximum(m, jnp.max(s, axis=1, keepdims=True))
        p = jnp.exp(s - m_new)
        if masked:
            p = jnp.where(visible, p, 0.0)
        alpha = jnp.exp(m - m_new)
        l_new = l * alpha + jnp.sum(p, axis=1, keepdims=True)
        acc_new = acc * alpha + lax.dot_general(
            p.astype(jnp.bfloat16), vals, (((1,), (1,)), ((), ())), preferred_element_type=jnp.float32
        )
        return (m_new, l_new, acc_new)

    if has_init:
        carry = (m_in[...], l_in[...], acc_in[...])
    else:
        carry = (
            jnp.full((BQ, 1), NEG, jnp.float32),
            jnp.zeros((BQ, 1), jnp.float32),
            jnp.zeros((BQ, HD), jnp.float32),
        )
    carry = lax.fori_loop(b0, b1, partial(step, masked=True), carry)
    carry = lax.fori_loop(b1, b2, partial(step, masked=False), carry)
    carry = lax.fori_loop(b2, b3, partial(step, masked=True), carry)
    m, l, acc = carry
    if finalize:
        (out_ref,) = rest
        out_ref[...] = (acc / l).astype(out_ref.dtype)
    else:
        m_out, l_out, acc_out = rest
        m_out[...] = m
        l_out[...] = l
        acc_out[...] = acc


def block_table(q_first_rows, lo_first, lo_last, key_offset, key_rows):
    q_last = q_first_rows + BQ - 1
    local_lo = jnp.clip(lo_first - key_offset, 0, key_rows)
    local_hi = jnp.clip(q_last + 1 - key_offset, 0, key_rows)
    b0 = local_lo // BK
    b3 = jnp.maximum((local_hi + BK - 1) // BK, b0)
    full_lo = (jnp.maximum(lo_last - key_offset, 0) + BK - 1) // BK
    full_hi = (q_first_rows + 1 - key_offset) // BK
    b1 = jnp.clip(full_lo, b0, b3)
    b2 = jnp.clip(full_hi, b1, b3)
    offsets = jnp.broadcast_to(key_offset, q_first_rows.shape)
    zero = jnp.zeros_like(b0)
    table = jnp.stack([b0, b1, b2, b3, q_first_rows, offsets, zero, zero], axis=1)
    return table.reshape(-1).astype(jnp.int32)


def attend(table, queries, lows, kv, state, finalize, source_rows):
    rows = queries.shape[0]
    grid = (rows // BQ,)
    row_spec = lambda width: pl.BlockSpec((BQ, width), lambda i, t: (i, 0))
    in_specs = [row_spec(HD), row_spec(1), pl.BlockSpec(kv.shape, lambda i, t: (0, 0, 0))]
    operands = [queries, lows, kv]
    if state is not None:
        in_specs += [row_spec(1), row_spec(1), row_spec(HD)]
        operands += list(state)
    if finalize:
        out_shape = jax.ShapeDtypeStruct((rows, HD), jnp.bfloat16)
        out_specs = row_spec(HD)
    else:
        out_shape = (
            jax.ShapeDtypeStruct((rows, 1), jnp.float32),
            jax.ShapeDtypeStruct((rows, 1), jnp.float32),
            jax.ShapeDtypeStruct((rows, HD), jnp.float32),
        )
        out_specs = (row_spec(1), row_spec(1), row_spec(HD))
    kernel = partial(attention_kernel, has_init=state is not None, finalize=finalize, per_source=source_rows // BK)
    return pl.pallas_call(
        kernel,
        grid_spec=pltpu.PrefetchScalarGridSpec(
            num_scalar_prefetch=1,
            grid=grid,
            in_specs=in_specs,
            out_specs=out_specs,
        ),
        out_shape=out_shape,
        compiler_params=pltpu.CompilerParams(vmem_limit_bytes=48 * 1024 * 1024),
    )(table, *operands)


def per_device(lengths, page_table, projected, residual, out_weight):
    row_count = projected.shape[0]
    local_heads = projected.shape[1] // (3 * HD)
    group_size = lax.axis_size("gx")
    group_index = lax.axis_index("gx")
    first_row = group_index * row_count
    ends_at = jnp.cumsum(lengths)
    starts_at = ends_at - lengths
    own_index = first_row + jnp.arange(row_count, dtype=jnp.int32)
    own_segment = segment_of(ends_at, own_index)
    own_position = own_index - starts_at[own_segment]
    split_heads = projected.reshape(row_count, local_heads, 3, HD)
    rotated_queries = rotate(split_heads[:, :, 0], own_position)
    rotated_keys = rotate(split_heads[:, :, 1], own_position)
    key_value = jnp.concatenate([rotated_keys, split_heads[:, :, 2]], axis=-1)
    queries = rotated_queries.reshape(row_count, HD)
    local_kv = key_value.reshape(row_count, 2 * HD)
    weight_rows = out_weight.reshape(-1, 2 * HD)
    stacked_rows = row_count + weight_rows.shape[0]
    gathered = lax.all_gather(jnp.concatenate([local_kv, weight_rows], axis=0), "gx", axis=0, tiled=True)
    gathered = gathered.reshape(group_size, stacked_rows, 2 * HD)
    weight_columns = gathered[:, row_count:].reshape(-1, out_weight.shape[1])
    key_count = group_size * row_count

    half = row_count // 2
    half_blocks = half // BQ
    lows = starts_at[own_segment]
    q_first_rows = first_row + jnp.arange(0, half, BQ, dtype=jnp.int32)
    lo_first = lows[0:half:BQ]
    lo_last = lows[BQ - 1 : half : BQ]
    lows = lows.reshape(row_count, 1)
    own_table = block_table(q_first_rows, lo_first, lo_last, first_row, row_count)
    state = attend(own_table, queries[:half], lows[:half], local_kv.T[None], None, False, row_count)

    partners = [(i, group_size - 1 - i) for i in range(group_size)]
    partner_queries = lax.ppermute(queries[half:], "gx", partners)
    partner_residual = lax.ppermute(residual[half:], "gx", partners)
    partner_first = (group_size - 1 - group_index) * row_count + half
    partner_index = partner_first + jnp.arange(half, dtype=jnp.int32)
    partner_lows = starts_at[segment_of(ends_at, partner_index)]
    partner_table = block_table(
        partner_first + jnp.arange(0, half, BQ, dtype=jnp.int32),
        partner_lows[0::BQ],
        partner_lows[BQ - 1 :: BQ],
        jnp.int32(0),
        key_count,
    )
    partner_lows = partner_lows.reshape(half, 1)

    tail_rows = passed_along(key_value[: PAGE - 1], "gx", -1)
    extended = jnp.concatenate([key_value, tail_rows], axis=0)
    extended_index = first_row + jnp.arange(row_count + PAGE - 1, dtype=jnp.int32)
    extended_segment = jnp.minimum(segment_of(ends_at, extended_index), lengths.shape[0] - 1)
    extended_position = extended_index - starts_at[extended_segment]
    page_count = (lengths + PAGE - 1) // PAGE
    page_base = jnp.cumsum(page_count) - page_count
    logical = page_base[extended_segment] + extended_position // PAGE
    page_first = extended_index - extended_position % PAGE
    pages_held = row_count // PAGE + lengths.shape[0]
    owned = (page_first // row_count == group_index) & (extended_index < group_size * row_count)
    target = jnp.where(owned, page_table[logical] - group_index * pages_held, pages_held)
    cache_pages = jnp.zeros((pages_held, local_heads, PAGE, 2 * HD), jnp.bfloat16)
    cache_pages = cache_pages.at[target, :, extended_position % PAGE].set(extended, mode="drop")

    key_columns = jnp.swapaxes(gathered, 1, 2)
    key_columns, cache_pages, state, partner_queries, partner_residual = lax.optimization_barrier(
        (key_columns, cache_pages, state, partner_queries, partner_residual)
    )
    rest_table = block_table(q_first_rows, lo_first, lo_last, jnp.int32(0), jnp.minimum(first_row, key_count))
    first_half = attend(rest_table, queries[:half], lows[:half], key_columns, state, True, row_count)
    partner_out = attend(partner_table, partner_queries, partner_lows, key_columns, None, True, row_count)

    both = jnp.concatenate([first_half, partner_out], axis=0)
    update = jnp.dot(
        lax.all_gather(both, "gy", axis=1, tiled=True),
        weight_columns,
        preferred_element_type=jnp.float32,
    )
    both_residual = jnp.concatenate([residual[:half], partner_residual], axis=0)
    projected = (both_residual.astype(jnp.float32) + update).astype(jnp.bfloat16)
    hidden_second = lax.ppermute(projected[half:], "gx", partners)
    hidden = jnp.concatenate([projected[:half], hidden_second], axis=0)
    return (hidden, cache_pages.reshape(pages_held, local_heads, PAGE * 2 * HD))


def solution(mesh):
    placed = (P(), P(), P("gx", "gy"), P("gx", "gy"), P("gx", "gy"))
    return jax.shard_map(
        per_device,
        mesh=mesh,
        in_specs=placed,
        out_specs=(P("gx", "gy"), P("gx", "gy", None)),
        check_vma=False,
    )
```

```python
from functools import partial
import math

import jax
import jax.numpy as jnp
from jax import lax
from jax.experimental import pallas as pl
from jax.experimental.pallas import tpu as pltpu
from jax.sharding import PartitionSpec as P

HD = 96
PAGE = 16
BQ = 384
BK = 384
NEG = -1e30


def passed_along(block, axis, distance):
    devices = range(lax.axis_size(axis))
    route = [(i - distance, i) for i in devices if i - distance in devices]
    return lax.ppermute(block, axis, route)


def segment_of(ends_at, token_index):
    return jnp.sum((ends_at[None, :] <= token_index[:, None]).astype(jnp.int32), axis=1)


def rotate(values, position):
    half_size = HD // 2
    inverse = 10000.0 ** (-(jnp.arange(half_size, dtype=jnp.float32) * 2.0) / HD)
    angle = position.astype(jnp.float32)[:, None, None] * inverse[None, None, :]
    cosine = jnp.cos(angle)
    sine_part = jnp.sin(angle)
    widened = values.astype(jnp.float32)
    front_half = widened[..., :half_size]
    back_half = widened[..., half_size:]
    turned = jnp.concatenate(
        [front_half * cosine - back_half * sine_part, back_half * cosine + front_half * sine_part],
        axis=-1,
    )
    return turned.astype(jnp.bfloat16)


def attention_kernel(table_ref, q_ref, lo_ref, kv_ref, *rest, has_init, finalize, per_source):
    if has_init:
        m_in, l_in, acc_in = rest[:3]
        rest = rest[3:]
    i = pl.program_id(0)
    b0 = table_ref[i * 8 + 0]
    b1 = table_ref[i * 8 + 1]
    b2 = table_ref[i * 8 + 2]
    b3 = table_ref[i * 8 + 3]
    q_first = table_ref[i * 8 + 4]
    key_offset = table_ref[i * 8 + 5]
    q = q_ref[...]
    lo = lo_ref[...]
    q_index = q_first + lax.broadcasted_iota(jnp.int32, (BQ, 1), 0)
    scale = 1.0 / math.sqrt(HD)

    def step(kb, carry, masked):
        m, l, acc = carry
        start = pl.multiple_of(kb * BK, BK)
        source = kb // per_source
        within = pl.multiple_of((kb % per_source) * BK, BK)
        keys = kv_ref[source, pl.ds(0, HD), pl.ds(within, BK)]
        vals = kv_ref[source, pl.ds(HD, HD), pl.ds(within, BK)]
        s = jnp.dot(q, keys, preferred_element_type=jnp.float32) * scale
        if masked:
            k_index = key_offset + start + lax.broadcasted_iota(jnp.int32, (1, BK), 1)
            visible = (k_index >= lo) & (k_index <= q_index)
            s = jnp.where(visible, s, NEG)
        m_new = jnp.maximum(m, jnp.max(s, axis=1, keepdims=True))
        p = jnp.exp(s - m_new)
        if masked:
            p = jnp.where(visible, p, 0.0)
        alpha = jnp.exp(m - m_new)
        l_new = l * alpha + jnp.sum(p, axis=1, keepdims=True)
        acc_new = acc * alpha + lax.dot_general(
            p.astype(jnp.bfloat16), vals, (((1,), (1,)), ((), ())), preferred_element_type=jnp.float32
        )
        return (m_new, l_new, acc_new)

    if has_init:
        carry = (m_in[...], l_in[...], acc_in[...])
    else:
        carry = (
            jnp.full((BQ, 1), NEG, jnp.float32),
            jnp.zeros((BQ, 1), jnp.float32),
            jnp.zeros((BQ, HD), jnp.float32),
        )
    carry = lax.fori_loop(b0, b1, partial(step, masked=True), carry)
    carry = lax.fori_loop(b1, b2, partial(step, masked=False), carry)
    carry = lax.fori_loop(b2, b3, partial(step, masked=True), carry)
    m, l, acc = carry
    if finalize:
        (out_ref,) = rest
        out_ref[...] = (acc / l).astype(out_ref.dtype)
    else:
        m_out, l_out, acc_out = rest
        m_out[...] = m
        l_out[...] = l
        acc_out[...] = acc


def block_table(q_first_rows, lo_first, lo_last, key_offset, key_rows):
    q_last = q_first_rows + BQ - 1
    local_lo = jnp.clip(lo_first - key_offset, 0, key_rows)
    local_hi = jnp.clip(q_last + 1 - key_offset, 0, key_rows)
    b0 = local_lo // BK
    b3 = jnp.maximum((local_hi + BK - 1) // BK, b0)
    full_lo = (jnp.maximum(lo_last - key_offset, 0) + BK - 1) // BK
    full_hi = (q_first_rows + 1 - key_offset) // BK
    b1 = jnp.clip(full_lo, b0, b3)
    b2 = jnp.clip(full_hi, b1, b3)
    offsets = jnp.broadcast_to(key_offset, q_first_rows.shape)
    zero = jnp.zeros_like(b0)
    table = jnp.stack([b0, b1, b2, b3, q_first_rows, offsets, zero, zero], axis=1)
    return table.reshape(-1).astype(jnp.int32)


def attend(table, queries, lows, kv, state, finalize, source_rows):
    rows = queries.shape[0]
    grid = (rows // BQ,)
    row_spec = lambda width: pl.BlockSpec((BQ, width), lambda i, t: (i, 0))
    in_specs = [row_spec(HD), row_spec(1), pl.BlockSpec(kv.shape, lambda i, t: (0, 0, 0))]
    operands = [queries, lows, kv]
    if state is not None:
        in_specs += [row_spec(1), row_spec(1), row_spec(HD)]
        operands += list(state)
    if finalize:
        out_shape = jax.ShapeDtypeStruct((rows, HD), jnp.bfloat16)
        out_specs = row_spec(HD)
    else:
        out_shape = (
            jax.ShapeDtypeStruct((rows, 1), jnp.float32),
            jax.ShapeDtypeStruct((rows, 1), jnp.float32),
            jax.ShapeDtypeStruct((rows, HD), jnp.float32),
        )
        out_specs = (row_spec(1), row_spec(1), row_spec(HD))
    kernel = partial(attention_kernel, has_init=state is not None, finalize=finalize, per_source=source_rows // BK)
    return pl.pallas_call(
        kernel,
        grid_spec=pltpu.PrefetchScalarGridSpec(
            num_scalar_prefetch=1,
            grid=grid,
            in_specs=in_specs,
            out_specs=out_specs,
        ),
        out_shape=out_shape,
        compiler_params=pltpu.CompilerParams(vmem_limit_bytes=48 * 1024 * 1024),
    )(table, *operands)


def per_device(lengths, page_table, projected, residual, out_weight):
    row_count = projected.shape[0]
    local_heads = projected.shape[1] // (3 * HD)
    group_size = lax.axis_size("gx")
    group_index = lax.axis_index("gx")
    first_row = group_index * row_count
    ends_at = jnp.cumsum(lengths)
    starts_at = ends_at - lengths
    own_index = first_row + jnp.arange(row_count, dtype=jnp.int32)
    own_segment = segment_of(ends_at, own_index)
    own_position = own_index - starts_at[own_segment]
    split_heads = projected.reshape(row_count, local_heads, 3, HD)
    rotated_queries = rotate(split_heads[:, :, 0], own_position)
    rotated_keys = rotate(split_heads[:, :, 1], own_position)
    key_value = jnp.concatenate([rotated_keys, split_heads[:, :, 2]], axis=-1)
    queries = rotated_queries.reshape(row_count, HD)
    local_kv = key_value.reshape(row_count, 2 * HD)
    weight_rows = out_weight.reshape(-1, 2 * HD)
    stacked_rows = row_count + weight_rows.shape[0]
    gathered = lax.all_gather(jnp.concatenate([local_kv, weight_rows], axis=0), "gx", axis=0, tiled=True)
    gathered = gathered.reshape(group_size, stacked_rows, 2 * HD)
    weight_columns = gathered[:, row_count:].reshape(-1, out_weight.shape[1])
    key_count = group_size * row_count

    half = row_count // 2
    half_blocks = half // BQ
    lows = starts_at[own_segment]
    q_first_rows = first_row + jnp.arange(0, half, BQ, dtype=jnp.int32)
    lo_first = lows[0:half:BQ]
    lo_last = lows[BQ - 1 : half : BQ]
    lows = lows.reshape(row_count, 1)
    own_table = block_table(q_first_rows, lo_first, lo_last, first_row, row_count)
    state = attend(own_table, queries[:half], lows[:half], local_kv.T[None], None, False, row_count)

    partners = [(i, group_size - 1 - i) for i in range(group_size)]
    partner_queries = lax.ppermute(queries[half:], "gx", partners)
    partner_residual = lax.ppermute(residual[half:], "gx", partners)
    partner_first = (group_size - 1 - group_index) * row_count + half
    partner_index = partner_first + jnp.arange(half, dtype=jnp.int32)
    partner_lows = starts_at[segment_of(ends_at, partner_index)]
    partner_table = block_table(
        partner_first + jnp.arange(0, half, BQ, dtype=jnp.int32),
        partner_lows[0::BQ],
        partner_lows[BQ - 1 :: BQ],
        jnp.int32(0),
        key_count,
    )
    partner_lows = partner_lows.reshape(half, 1)

    tail_rows = passed_along(key_value[: PAGE - 1], "gx", -1)
    extended = jnp.concatenate([key_value, tail_rows], axis=0)
    extended_index = first_row + jnp.arange(row_count + PAGE - 1, dtype=jnp.int32)
    extended_segment = jnp.minimum(segment_of(ends_at, extended_index), lengths.shape[0] - 1)
    extended_position = extended_index - starts_at[extended_segment]
    page_count = (lengths + PAGE - 1) // PAGE
    page_base = jnp.cumsum(page_count) - page_count
    logical = page_base[extended_segment] + extended_position // PAGE
    page_first = extended_index - extended_position % PAGE
    pages_held = row_count // PAGE + lengths.shape[0]
    owned = (page_first // row_count == group_index) & (extended_index < group_size * row_count)
    target = jnp.where(owned, page_table[logical] - group_index * pages_held, pages_held)
    cache_pages = jnp.zeros((pages_held, local_heads, PAGE, 2 * HD), jnp.bfloat16)
    cache_pages = cache_pages.at[target, :, extended_position % PAGE].set(extended, mode="drop")

    key_columns = jnp.swapaxes(gathered, 1, 2)
    key_columns, cache_pages, state, partner_queries, partner_residual = lax.optimization_barrier(
        (key_columns, cache_pages, state, partner_queries, partner_residual)
    )
    rest_table = block_table(q_first_rows, lo_first, lo_last, jnp.int32(0), jnp.minimum(first_row, key_count))
    first_half = attend(rest_table, queries[:half], lows[:half], key_columns, state, True, row_count)
    partner_out = attend(partner_table, partner_queries, partner_lows, key_columns, None, True, row_count)

    both = jnp.concatenate([first_half, partner_out], axis=0)
    update = jnp.dot(
        lax.all_gather(both, "gy", axis=1, tiled=True),
        weight_columns,
        preferred_element_type=jnp.float32,
    )
    both_residual = jnp.concatenate([residual[:half], partner_residual], axis=0)
    projected = (both_residual.astype(jnp.float32) + update).astype(jnp.bfloat16)
    hidden_second = lax.ppermute(projected[half:], "gx", partners)
    hidden = jnp.concatenate([projected[:half], hidden_second], axis=0)
    return (hidden, cache_pages.reshape(pages_held, local_heads, PAGE * 2 * HD))


def solution(mesh):
    placed = (P(), P(), P("gx", "gy"), P("gx", "gy"), P("gx", "gy"))
    return jax.shard_map(
        per_device,
        mesh=mesh,
        in_specs=placed,
        out_specs=(P("gx", "gy"), P("gx", "gy", None)),
        check_vma=False,
    )
```

```python
from functools import partial
import math

import jax
import jax.numpy as jnp
from jax import lax
from jax.experimental import pallas as pl
from jax.experimental.pallas import tpu as pltpu
from jax.sharding import PartitionSpec as P

HD = 96
PAGE = 16
BQ = 384
BK = 768
NEG = -1e30


def passed_along(block, axis, distance):
    devices = range(lax.axis_size(axis))
    route = [(i - distance, i) for i in devices if i - distance in devices]
    return lax.ppermute(block, axis, route)


def segment_of(ends_at, token_index):
    return jnp.sum((ends_at[None, :] <= token_index[:, None]).astype(jnp.int32), axis=1)


def rotate(values, position):
    half_size = HD // 2
    inverse = 10000.0 ** (-(jnp.arange(half_size, dtype=jnp.float32) * 2.0) / HD)
    angle = position.astype(jnp.float32)[:, None, None] * inverse[None, None, :]
    cosine = jnp.cos(angle)
    sine_part = jnp.sin(angle)
    widened = values.astype(jnp.float32)
    front_half = widened[..., :half_size]
    back_half = widened[..., half_size:]
    turned = jnp.concatenate(
        [front_half * cosine - back_half * sine_part, back_half * cosine + front_half * sine_part],
        axis=-1,
    )
    return turned.astype(jnp.bfloat16)


def attention_kernel(table_ref, q_ref, lo_ref, kv_ref, *rest, has_init, finalize, per_source):
    if has_init:
        m_in, l_in, acc_in = rest[:3]
        rest = rest[3:]
    i = pl.program_id(0)
    b0 = table_ref[i * 8 + 0]
    b1 = table_ref[i * 8 + 1]
    b2 = table_ref[i * 8 + 2]
    b3 = table_ref[i * 8 + 3]
    q_first = table_ref[i * 8 + 4]
    key_offset = table_ref[i * 8 + 5]
    q = q_ref[...]
    lo = lo_ref[...]
    q_index = q_first + lax.broadcasted_iota(jnp.int32, (BQ, 1), 0)
    scale = 1.0 / math.sqrt(HD)

    def step(kb, carry, masked):
        m, l, acc = carry
        start = pl.multiple_of(kb * BK, BK)
        source = kb // per_source
        within = pl.multiple_of((kb % per_source) * BK, BK)
        keys = kv_ref[source, pl.ds(0, HD), pl.ds(within, BK)]
        vals = kv_ref[source, pl.ds(HD, HD), pl.ds(within, BK)]
        s = jnp.dot(q, keys, preferred_element_type=jnp.float32) * scale
        if masked:
            k_index = key_offset + start + lax.broadcasted_iota(jnp.int32, (1, BK), 1)
            visible = (k_index >= lo) & (k_index <= q_index)
            s = jnp.where(visible, s, NEG)
        m_new = jnp.maximum(m, jnp.max(s, axis=1, keepdims=True))
        p = jnp.exp(s - m_new)
        if masked:
            p = jnp.where(visible, p, 0.0)
        alpha = jnp.exp(m - m_new)
        l_new = l * alpha + jnp.sum(p, axis=1, keepdims=True)
        acc_new = acc * alpha + lax.dot_general(
            p.astype(jnp.bfloat16), vals, (((1,), (1,)), ((), ())), preferred_element_type=jnp.float32
        )
        return (m_new, l_new, acc_new)

    if has_init:
        carry = (m_in[...], l_in[...], acc_in[...])
    else:
        carry = (
            jnp.full((BQ, 1), NEG, jnp.float32),
            jnp.zeros((BQ, 1), jnp.float32),
            jnp.zeros((BQ, HD), jnp.float32),
        )
    carry = lax.fori_loop(b0, b1, partial(step, masked=True), carry)
    carry = lax.fori_loop(b1, b2, partial(step, masked=False), carry)
    carry = lax.fori_loop(b2, b3, partial(step, masked=True), carry)
    m, l, acc = carry
    if finalize:
        (out_ref,) = rest
        out_ref[...] = (acc / l).astype(out_ref.dtype)
    else:
        m_out, l_out, acc_out = rest
        m_out[...] = m
        l_out[...] = l
        acc_out[...] = acc


def block_table(q_first_rows, lo_first, lo_last, key_offset, key_rows):
    q_last = q_first_rows + BQ - 1
    local_lo = jnp.clip(lo_first - key_offset, 0, key_rows)
    local_hi = jnp.clip(q_last + 1 - key_offset, 0, key_rows)
    b0 = local_lo // BK
    b3 = jnp.maximum((local_hi + BK - 1) // BK, b0)
    full_lo = (jnp.maximum(lo_last - key_offset, 0) + BK - 1) // BK
    full_hi = (q_first_rows + 1 - key_offset) // BK
    b1 = jnp.clip(full_lo, b0, b3)
    b2 = jnp.clip(full_hi, b1, b3)
    offsets = jnp.broadcast_to(key_offset, q_first_rows.shape)
    zero = jnp.zeros_like(b0)
    table = jnp.stack([b0, b1, b2, b3, q_first_rows, offsets, zero, zero], axis=1)
    return table.reshape(-1).astype(jnp.int32)


def attend(table, queries, lows, kv, state, finalize, source_rows):
    rows = queries.shape[0]
    grid = (rows // BQ,)
    row_spec = lambda width: pl.BlockSpec((BQ, width), lambda i, t: (i, 0))
    in_specs = [row_spec(HD), row_spec(1), pl.BlockSpec(kv.shape, lambda i, t: (0, 0, 0))]
    operands = [queries, lows, kv]
    if state is not None:
        in_specs += [row_spec(1), row_spec(1), row_spec(HD)]
        operands += list(state)
    if finalize:
        out_shape = jax.ShapeDtypeStruct((rows, HD), jnp.bfloat16)
        out_specs = row_spec(HD)
    else:
        out_shape = (
            jax.ShapeDtypeStruct((rows, 1), jnp.float32),
            jax.ShapeDtypeStruct((rows, 1), jnp.float32),
            jax.ShapeDtypeStruct((rows, HD), jnp.float32),
        )
        out_specs = (row_spec(1), row_spec(1), row_spec(HD))
    kernel = partial(attention_kernel, has_init=state is not None, finalize=finalize, per_source=source_rows // BK)
    return pl.pallas_call(
        kernel,
        grid_spec=pltpu.PrefetchScalarGridSpec(
            num_scalar_prefetch=1,
            grid=grid,
            in_specs=in_specs,
            out_specs=out_specs,
        ),
        out_shape=out_shape,
        compiler_params=pltpu.CompilerParams(vmem_limit_bytes=48 * 1024 * 1024),
    )(table, *operands)


def per_device(lengths, page_table, projected, residual, out_weight):
    row_count = projected.shape[0]
    local_heads = projected.shape[1] // (3 * HD)
    group_size = lax.axis_size("gx")
    group_index = lax.axis_index("gx")
    first_row = group_index * row_count
    ends_at = jnp.cumsum(lengths)
    starts_at = ends_at - lengths
    own_index = first_row + jnp.arange(row_count, dtype=jnp.int32)
    own_segment = segment_of(ends_at, own_index)
    own_position = own_index - starts_at[own_segment]
    split_heads = projected.reshape(row_count, local_heads, 3, HD)
    rotated_queries = rotate(split_heads[:, :, 0], own_position)
    rotated_keys = rotate(split_heads[:, :, 1], own_position)
    key_value = jnp.concatenate([rotated_keys, split_heads[:, :, 2]], axis=-1)
    queries = rotated_queries.reshape(row_count, HD)
    local_kv = key_value.reshape(row_count, 2 * HD)
    weight_rows = out_weight.reshape(-1, 2 * HD)
    stacked_rows = row_count + weight_rows.shape[0]
    gathered = lax.all_gather(jnp.concatenate([local_kv, weight_rows], axis=0), "gx", axis=0, tiled=True)
    gathered = gathered.reshape(group_size, stacked_rows, 2 * HD)
    weight_columns = gathered[:, row_count:].reshape(-1, out_weight.shape[1])
    key_count = group_size * row_count

    half = row_count // 2
    half_blocks = half // BQ
    lows = starts_at[own_segment]
    q_first_rows = first_row + jnp.arange(0, half, BQ, dtype=jnp.int32)
    lo_first = lows[0:half:BQ]
    lo_last = lows[BQ - 1 : half : BQ]
    lows = lows.reshape(row_count, 1)
    own_table = block_table(q_first_rows, lo_first, lo_last, first_row, row_count)
    state = attend(own_table, queries[:half], lows[:half], local_kv.T[None], None, False, row_count)

    partners = [(i, group_size - 1 - i) for i in range(group_size)]
    partner_queries = lax.ppermute(queries[half:], "gx", partners)
    partner_residual = lax.ppermute(residual[half:], "gx", partners)
    partner_first = (group_size - 1 - group_index) * row_count + half
    partner_index = partner_first + jnp.arange(half, dtype=jnp.int32)
    partner_lows = starts_at[segment_of(ends_at, partner_index)]
    partner_table = block_table(
        partner_first + jnp.arange(0, half, BQ, dtype=jnp.int32),
        partner_lows[0::BQ],
        partner_lows[BQ - 1 :: BQ],
        jnp.int32(0),
        key_count,
    )
    partner_lows = partner_lows.reshape(half, 1)

    tail_rows = passed_along(key_value[: PAGE - 1], "gx", -1)
    extended = jnp.concatenate([key_value, tail_rows], axis=0)
    extended_index = first_row + jnp.arange(row_count + PAGE - 1, dtype=jnp.int32)
    extended_segment = jnp.minimum(segment_of(ends_at, extended_index), lengths.shape[0] - 1)
    extended_position = extended_index - starts_at[extended_segment]
    page_count = (lengths + PAGE - 1) // PAGE
    page_base = jnp.cumsum(page_count) - page_count
    logical = page_base[extended_segment] + extended_position // PAGE
    page_first = extended_index - extended_position % PAGE
    pages_held = row_count // PAGE + lengths.shape[0]
    owned = (page_first // row_count == group_index) & (extended_index < group_size * row_count)
    target = jnp.where(owned, page_table[logical] - group_index * pages_held, pages_held)
    cache_pages = jnp.zeros((pages_held, local_heads, PAGE, 2 * HD), jnp.bfloat16)
    cache_pages = cache_pages.at[target, :, extended_position % PAGE].set(extended, mode="drop")

    key_columns = jnp.swapaxes(gathered, 1, 2)
    key_columns, cache_pages, state, partner_queries, partner_residual = lax.optimization_barrier(
        (key_columns, cache_pages, state, partner_queries, partner_residual)
    )
    rest_table = block_table(q_first_rows, lo_first, lo_last, jnp.int32(0), jnp.minimum(first_row, key_count))
    fresh = (
        jnp.full((half, 1), NEG, jnp.float32),
        jnp.zeros((half, 1), jnp.float32),
        jnp.zeros((half, HD), jnp.float32),
    )
    both = attend(
        jnp.concatenate([rest_table, partner_table]),
        jnp.concatenate([queries[:half], partner_queries], axis=0),
        jnp.concatenate([lows[:half], partner_lows], axis=0),
        key_columns,
        tuple(jnp.concatenate([mine, new], axis=0) for mine, new in zip(state, fresh)),
        True,
        row_count,
    )
    update = jnp.dot(
        lax.all_gather(both, "gy", axis=1, tiled=True),
        weight_columns,
        preferred_element_type=jnp.float32,
    )
    both_residual = jnp.concatenate([residual[:half], partner_residual], axis=0)
    projected = (both_residual.astype(jnp.float32) + update).astype(jnp.bfloat16)
    hidden_second = lax.ppermute(projected[half:], "gx", partners)
    hidden = jnp.concatenate([projected[:half], hidden_second], axis=0)
    return (hidden, cache_pages.reshape(pages_held, local_heads, PAGE * 2 * HD))


def solution(mesh):
    placed = (P(), P(), P("gx", "gy"), P("gx", "gy"), P("gx", "gy"))
    return jax.shard_map(
        per_device,
        mesh=mesh,
        in_specs=placed,
        out_specs=(P("gx", "gy"), P("gx", "gy", None)),
        check_vma=False,
    )
```
